128 devices in a mesh: seq: 16 (over z_hi, y, core), chan: 8 (over x, z_lo).
Axes of the slice: x: 4, y: 4, z: 4 (z_hi: 2, z_lo: 2; z = z_hi * 2 + z_lo), core: 2. Of those that a mesh axis runs over, the one named last changes fastest.
Arguments:
- query_rows: bfloat16 [2048, 8192], P('seq', 'chan'), may hold values from -6 to 6
- key_rows: bfloat16 [2048, 8192], P('seq', 'chan'), may hold values from -6 to 6
- value_rows: bfloat16 [2048, 8192], P('seq', 'chan'), may hold values from -6 to 6
- grad_rows: bfloat16 [2048, 8192], P('seq', 'chan'), may hold values from -21 to 21
- filters: bfloat16 [512, 128], P('chan'), may hold values from -0.5 to 0.5
- span_order: int32 [32], replicated, may hold values from 0 to 31, as said below
Outputs:
- gated_out: bfloat16 [2048, 8192], P('seq', 'chan')
- grad_query: bfloat16 [2048, 8192], P('seq', 'chan')
- grad_key: bfloat16 [2048, 8192], P('seq', 'chan')
- grad_value: bfloat16 [2048, 8192], P('seq', 'chan')
- filter_grad: float32 [512, 128], P('chan')
The draws below stay inside these ranges and needn't reach their ends.
Inputs may be any that keep to these rules, and one draw needn't show every extreme that they name: span_order names every span once. Slot s lies on seq index s // 2, and span c is owned by seq index c // 2. Seq index i holds a span p below 16 in slot 2 * i and span 32 - 1 - p in slot 2 * i + 1; which p each index holds is drawn. No seq index holds two spans of one owner.
All inputs are finite; a program needn't handle non-finite values.
Results may differ from the reference program's by a relative error of at most 0.0085.
Values may be sent and summed in bfloat16 or wider, within the bound.
No kernel may reach another device: no remote copies, remote signals or barrier semaphores. Data moves between devices by JAX's collectives and lax.ppermute only.
A program may use at most 128 MiB of HBM per device.

```python
import math
import jax
import jax.numpy as jnp
import numpy as np
from jax import lax

D = 8192
GROUP = 16
K = 128
GROUPS = 512
SPAN_ROWS = 64
TOKENS = 2048
SPANS = 32
N_SEQ = 16


def draw_grad_rows(key, part):
    first_key = jax.random.fold_in(key, 0)
    column = jnp.arange(D, dtype=jnp.float32) / D
    spread = jnp.power(10.0, column) / 3.0
    base = jnp.clip(jax.random.normal(first_key, (TOKENS, D), jnp.float32), -6.0, 6.0)
    values = base * spread[None, :]
    return values.astype(jnp.bfloat16)


def draw_span_order(key, part):
    order_key = jax.random.fold_in(key, 7)
    first = jax.random.permutation(order_key, jnp.arange(N_SEQ, dtype=jnp.int32)).astype(jnp.int32)
    second = (SPANS - 1 - first).astype(jnp.int32)
    return jnp.stack([first, second], axis=1).reshape(-1).astype(jnp.int32)


def block_levels(stream_key, shape, cuts, least, largest):
    factor_of, own = 1.0, jax.random.fold_in(stream_key, 6)
    for axis_at, parts in cuts:
        steps = jnp.exp(jax.random.uniform(jax.random.fold_in(own, axis_at), (parts,), jnp.float32, least / len(cuts), largest / len(cuts)))
        factor_of = factor_of * jnp.repeat(steps, shape[axis_at] // parts).reshape([-1 if axis == axis_at else 1 for axis in range(len(shape))])
    return factor_of


def normal_values(rng, shape, width, most, shards=(), kind=jnp.bfloat16):
    result = width * jax.random.normal(rng, shape, jnp.float32)
    if shards:
        result = result * block_levels(rng, shape, shards, -0.22, 0.18)
    return jnp.clip(result, -most, most).astype(kind)


def setup_inputs(seed: int = 0) -> dict:
    arg_keys = jax.random.split(jax.random.key(seed), 7)
    return {
        "query_rows": normal_values(arg_keys[0], (TOKENS, D), 1.0, 6.0, ((0, 16), (1, 8))),
        "key_rows": normal_values(arg_keys[1], (TOKENS, D), 1.0, 6.0, ((0, 16), (1, 8))),
        "value_rows": normal_values(arg_keys[2], (TOKENS, D), 1.0, 6.0, ((0, 16), (1, 8))),
        "grad_rows": draw_grad_rows(jax.random.fold_in(arg_keys[6], 71), 0),
        "filters": normal_values(arg_keys[4], (GROUPS, K), K ** -0.5, 0.5, ((0, 8),)),
        "span_order": draw_span_order(jax.random.fold_in(arg_keys[6], 71), 0),
    }


def band_tables(filters):
    taps = filters.shape[1]
    offsets = (np.arange(taps)[:, None] - np.arange(taps)[None, :]) % taps
    below = np.arange(taps)[:, None] >= np.arange(taps)[None, :]
    lookup = filters.astype(jnp.float32)[:, offsets]
    zeroed = jnp.zeros_like(lookup)
    return (jnp.where(below, lookup, zeroed), jnp.where(below, zeroed, lookup))

def times_rounded(left, right):
    return (left.astype(jnp.float32) * right.astype(jnp.float32)).astype(jnp.bfloat16)

def reference(query_rows, key_rows, value_rows, grad_rows, filters, span_order):

    def to_sequence(block):
        pieces = block.reshape(SPANS, SPAN_ROWS, D)
        return jnp.zeros_like(pieces).at[span_order].set(pieces).reshape(TOKENS, D)

    def to_slots(block):
        return block.reshape(SPANS, SPAN_ROWS, D)[span_order].reshape(TOKENS, D)
    highest = lax.Precision.HIGHEST
    queries = to_sequence(query_rows)
    keys_seq = to_sequence(key_rows)
    values_seq = to_sequence(value_rows)
    grads_seq = to_sequence(grad_rows)
    mixed_kv = times_rounded(keys_seq, values_seq)
    gated_grad = times_rounded(grads_seq, queries)
    main_band, wrap_band = band_tables(filters)
    zero_rows = jnp.zeros((K, D), jnp.float32)
    z_tiles = jnp.concatenate([zero_rows, mixed_kv.astype(jnp.float32)], axis=0).reshape(TOKENS // K + 1, K, GROUPS, GROUP)
    w_tiles = jnp.concatenate([gated_grad.astype(jnp.float32), zero_rows], axis=0).reshape(TOKENS // K + 1, K, GROUPS, GROUP)
    conv = jnp.einsum('gab,tbgc->tagc', main_band, z_tiles[1:], precision=highest)
    conv = conv + jnp.einsum('gab,tbgc->tagc', wrap_band, z_tiles[:-1], precision=highest)
    convolved = conv.reshape(TOKENS, D).astype(jnp.bfloat16)
    adjoint = jnp.einsum('gba,tbgc->tagc', main_band, w_tiles[:-1], precision=highest)
    adjoint = adjoint + jnp.einsum('gba,tbgc->tagc', wrap_band, w_tiles[1:], precision=highest)
    dmixed = adjoint.reshape(TOKENS, D).astype(jnp.bfloat16)
    main_corr = jnp.einsum('tagc,tbgc->gab', w_tiles[:-1], z_tiles[1:], precision=highest)
    wrap_corr = jnp.einsum('tagc,tbgc->gab', w_tiles[:-1], z_tiles[:-1], precision=highest)
    lag = np.arange(K)
    pick_main = (lag[:, None, None] - lag[None, :, None] == lag[None, None, :]).astype(np.float32)
    pick_wrap = (lag[:, None, None] - lag[None, :, None] + K == lag[None, None, :]).astype(np.float32)
    raw = jnp.einsum('gab,abj->gj', main_corr, jnp.asarray(pick_main, main_corr.dtype), precision=highest)
    raw = raw + jnp.einsum('gab,abj->gj', wrap_corr, jnp.asarray(pick_wrap, wrap_corr.dtype), precision=highest)
    squares = jnp.sum(raw * raw)
    limit = math.sqrt(GROUPS * K)
    factor = jnp.minimum(1.0, limit / jnp.sqrt(squares + 1e-06))
    filter_grad = factor * raw
    gated_out = to_slots(times_rounded(queries, convolved))
    grad_query = to_slots(times_rounded(grads_seq, convolved))
    grad_key = to_slots(times_rounded(dmixed, values_seq))
    grad_value = to_slots(times_rounded(dmixed, keys_seq))
    return (gated_out, grad_query, grad_key, grad_value, filter_grad)
```

```python
import math

import jax
import jax.numpy as jnp
from jax import lax
from jax.sharding import PartitionSpec as P


def times_rounded(left, right):
    return (left.astype(jnp.float32) * right.astype(jnp.float32)).astype(jnp.bfloat16)


def band_select(taps, out_rows, window, lead):
    j = lax.broadcasted_iota(jnp.int32, (taps, out_rows, window), 0)
    a = lax.broadcasted_iota(jnp.int32, (taps, out_rows, window), 1)
    w = lax.broadcasted_iota(jnp.int32, (taps, out_rows, window), 2)
    return (w == lead + a - j).astype(jnp.bfloat16)


def shards(query_rows, key_rows, value_rows, grad_rows, filters, span_order):
    device = lax.axis_index("seq")
    devices = lax.axis_size("seq")
    rows, channels = query_rows.shape
    spans = span_order.shape[0]
    span_rows = rows * devices // spans
    per_device = rows // span_rows
    taps = filters.shape[1]
    groups = filters.shape[0]
    group_size = channels // groups
    halo = -(-(taps - 1) // span_rows)
    lead = halo * span_rows
    window = lead + span_rows

    mixed = times_rounded(key_rows, value_rows)
    gated = times_rounded(grad_rows, query_rows)
    gathered = lax.all_gather(jnp.stack([mixed, gated]), "seq", axis=0, tiled=False)
    mixed_blocks = gathered[:, 0].reshape(spans, span_rows, channels)
    gated_blocks = gathered[:, 1].reshape(spans, span_rows, channels)

    slot_of = jnp.zeros((spans,), jnp.int32).at[span_order].set(jnp.arange(spans, dtype=jnp.int32))
    mine = lax.dynamic_slice_in_dim(span_order, device * per_device, per_device)
    step = jnp.arange(halo, dtype=jnp.int32)
    before = mine[:, None] - halo + step[None, :]
    after = mine[:, None] + 1 + step[None, :]

    def pick(blocks, wanted):
        valid = (wanted >= 0) & (wanted < spans)
        slots = slot_of[jnp.clip(wanted, 0, spans - 1)].reshape(-1)
        taken = jnp.take(blocks, slots, axis=0).reshape(per_device, halo, span_rows, channels)
        return jnp.where(valid[:, :, None, None], taken, jnp.zeros_like(taken))

    own_mixed = mixed.reshape(per_device, span_rows, channels)
    own_gated = gated.reshape(per_device, span_rows, channels)
    mixed_window = jnp.concatenate(
        [pick(mixed_blocks, before).reshape(per_device, lead, channels), own_mixed], axis=1
    )
    gated_window = jnp.concatenate(
        [own_gated, pick(gated_blocks, after).reshape(per_device, lead, channels)], axis=1
    )
    mixed_window = mixed_window.reshape(per_device, window, groups, group_size)
    gated_window = gated_window.reshape(per_device, window, groups, group_size)

    select_fwd = band_select(taps, span_rows, window, lead)
    fwd_band = jnp.einsum(
        "gj,jaw->gaw", filters, select_fwd, preferred_element_type=jnp.float32
    ).astype(jnp.bfloat16)
    bwd_band = jnp.einsum(
        "gj,jau->gau", filters, _bwd_select(taps, span_rows, window),
        preferred_element_type=jnp.float32,
    ).astype(jnp.bfloat16)

    conv = jnp.einsum("gaw,swgc->sagc", fwd_band, mixed_window, preferred_element_type=jnp.float32)
    convolved = conv.reshape(rows, channels).astype(jnp.bfloat16)
    adjoint = jnp.einsum("gau,sugc->sagc", bwd_band, gated_window, preferred_element_type=jnp.float32)
    dmixed = adjoint.reshape(rows, channels).astype(jnp.bfloat16)

    own_gated_g = own_gated.reshape(per_device, span_rows, groups, group_size)
    corr = jnp.einsum(
        "sagc,swgc->gaw", own_gated_g, mixed_window, preferred_element_type=jnp.float32
    )
    partial_grad = jnp.einsum(
        "gaw,jaw->gj", corr, select_fwd.astype(jnp.float32), precision=lax.Precision.HIGHEST
    )
    total_grad = lax.psum(partial_grad, "seq")
    squares = lax.psum(jnp.sum(total_grad * total_grad), "chan")
    limit = math.sqrt(groups * lax.axis_size("chan") * taps)
    factor = jnp.minimum(1.0, limit / jnp.sqrt(squares + 1e-06))
    filter_grad = factor * total_grad

    gated_out = times_rounded(query_rows, convolved)
    grad_query = times_rounded(grad_rows, convolved)
    grad_key = times_rounded(dmixed, value_rows)
    grad_value = times_rounded(dmixed, key_rows)
    return (gated_out, grad_query, grad_key, grad_value, filter_grad)


def _bwd_select(taps, out_rows, window):
    j = lax.broadcasted_iota(jnp.int32, (taps, out_rows, window), 0)
    a = lax.broadcasted_iota(jnp.int32, (taps, out_rows, window), 1)
    u = lax.broadcasted_iota(jnp.int32, (taps, out_rows, window), 2)
    return (u == a + j).astype(jnp.bfloat16)


def solution(mesh):
    return jax.shard_map(
        shards,
        mesh=mesh,
        in_specs=(
            P("seq", "chan"),
            P("seq", "chan"),
            P("seq", "chan"),
            P("seq", "chan"),
            P("chan", None),
            P(),
        ),
        out_specs=(
            P("seq", "chan"),
            P("seq", "chan"),
            P("seq", "chan"),
            P("seq", "chan"),
            P("chan", None),
        ),
        check_vma=False,
    )
```

```python
import math

import jax
import jax.numpy as jnp
from jax import lax
from jax.sharding import PartitionSpec as P


def times_rounded(left, right):
    return (left.astype(jnp.float32) * right.astype(jnp.float32)).astype(jnp.bfloat16)


def band_select(taps, out_rows, window, lead):
    j = lax.broadcasted_iota(jnp.int32, (taps, out_rows, window), 0)
    a = lax.broadcasted_iota(jnp.int32, (taps, out_rows, window), 1)
    w = lax.broadcasted_iota(jnp.int32, (taps, out_rows, window), 2)
    return (w == lead + a - j).astype(jnp.bfloat16)


def shards(query_rows, key_rows, value_rows, grad_rows, filters, span_order):
    device = lax.axis_index("seq")
    devices = lax.axis_size("seq")
    rows, channels = query_rows.shape
    spans = span_order.shape[0]
    span_rows = rows * devices // spans
    per_device = rows // span_rows
    taps = filters.shape[1]
    groups = filters.shape[0]
    group_size = channels // groups
    halo = -(-(taps - 1) // span_rows)
    lead = halo * span_rows
    window = lead + span_rows

    mixed = times_rounded(key_rows, value_rows)
    gated = times_rounded(grad_rows, query_rows)
    gathered = lax.all_gather(jnp.stack([mixed, gated]), "seq", axis=0, tiled=False)
    mixed_blocks = gathered[:, 0].reshape(spans, span_rows, channels)
    gated_blocks = gathered[:, 1].reshape(spans, span_rows, channels)

    slot_of = jnp.zeros((spans,), jnp.int32).at[span_order].set(jnp.arange(spans, dtype=jnp.int32))
    mine = lax.dynamic_slice_in_dim(span_order, device * per_device, per_device)
    step = jnp.arange(halo, dtype=jnp.int32)
    before = mine[:, None] - halo + step[None, :]
    after = mine[:, None] + 1 + step[None, :]

    def pick(blocks, wanted):
        valid = (wanted >= 0) & (wanted < spans)
        slots = slot_of[jnp.clip(wanted, 0, spans - 1)].reshape(-1)
        taken = jnp.take(blocks, slots, axis=0).reshape(per_device, halo, span_rows, channels)
        return jnp.where(valid[:, :, None, None], taken, jnp.zeros_like(taken))

    own_mixed = mixed.reshape(per_device, span_rows, channels)
    own_gated = gated.reshape(per_device, span_rows, channels)
    mixed_window = jnp.concatenate(
        [pick(mixed_blocks, before).reshape(per_device, lead, channels), own_mixed], axis=1
    )
    gated_window = jnp.concatenate(
        [own_gated, pick(gated_blocks, after).reshape(per_device, lead, channels)], axis=1
    )
    mixed_window = mixed_window.reshape(per_device, window, groups, group_size)
    gated_window = gated_window.reshape(per_device, window, groups, group_size)

    select_fwd = band_select(taps, span_rows, window, lead)
    fwd_band = jnp.einsum(
        "gj,jaw->gaw", filters, select_fwd, preferred_element_type=jnp.float32
    ).astype(jnp.bfloat16)
    bwd_band = jnp.einsum(
        "gj,jau->gau", filters, _bwd_select(taps, span_rows, window),
        preferred_element_type=jnp.float32,
    ).astype(jnp.bfloat16)

    conv = jnp.einsum("gaw,swgc->sagc", fwd_band, mixed_window, preferred_element_type=jnp.float32)
    convolved = conv.reshape(rows, channels).astype(jnp.bfloat16)
    adjoint = jnp.einsum("gau,sugc->sagc", bwd_band, gated_window, preferred_element_type=jnp.float32)
    dmixed = adjoint.reshape(rows, channels).astype(jnp.bfloat16)

    own_gated_g = own_gated.reshape(per_device, span_rows, groups, group_size)
    corr = jnp.einsum(
        "sagc,swgc->gaw", own_gated_g, mixed_window, preferred_element_type=jnp.float32
    )
    partial_grad = jnp.einsum(
        "gaw,jaw->gj", corr, select_fwd.astype(jnp.float32), precision=lax.Precision.HIGHEST
    )
    lanes = lax.axis_size("chan")
    slot = lax.axis_index("chan")
    placed = jnp.where(
        (jnp.arange(lanes) == slot)[:, None, None], partial_grad[None], jnp.zeros_like(partial_grad)[None]
    )
    every_grad = lax.psum(placed, ("seq", "chan"))
    squares = jnp.sum(every_grad * every_grad)
    limit = math.sqrt(groups * lanes * taps)
    factor = jnp.minimum(1.0, limit / jnp.sqrt(squares + 1e-06))
    total_grad = lax.dynamic_index_in_dim(every_grad, slot, 0, keepdims=False)
    filter_grad = factor * total_grad

    gated_out = times_rounded(query_rows, convolved)
    grad_query = times_rounded(grad_rows, convolved)
    grad_key = times_rounded(dmixed, value_rows)
    grad_value = times_rounded(dmixed, key_rows)
    return (gated_out, grad_query, grad_key, grad_value, filter_grad)


def _bwd_select(taps, out_rows, window):
    j = lax.broadcasted_iota(jnp.int32, (taps, out_rows, window), 0)
    a = lax.broadcasted_iota(jnp.int32, (taps, out_rows, window), 1)
    u = lax.broadcasted_iota(jnp.int32, (taps, out_rows, window), 2)
    return (u == a + j).astype(jnp.bfloat16)


def solution(mesh):
    return jax.shard_map(
        shards,
        mesh=mesh,
        in_specs=(
            P("seq", "chan"),
            P("seq", "chan"),
            P("seq", "chan"),
            P("seq", "chan"),
            P("chan", None),
            P(),
        ),
        out_specs=(
            P("seq", "chan"),
            P("seq", "chan"),
            P("seq", "chan"),
            P("seq", "chan"),
            P("chan", None),
        ),
        check_vma=False,
    )
```

```python
import math

import jax
import jax.numpy as jnp
from jax import lax
from jax.sharding import PartitionSpec as P


def times_rounded(left, right):
    return (left.astype(jnp.float32) * right.astype(jnp.float32)).astype(jnp.bfloat16)


def band_select(taps, out_rows, window, lead):
    j = lax.broadcasted_iota(jnp.int32, (taps, out_rows, window), 0)
    a = lax.broadcasted_iota(jnp.int32, (taps, out_rows, window), 1)
    w = lax.broadcasted_iota(jnp.int32, (taps, out_rows, window), 2)
    return (w == lead + a - j).astype(jnp.bfloat16)


def shards(query_rows, key_rows, value_rows, grad_rows, filters, span_order):
    device = lax.axis_index(SEQ)
    devices = lax.axis_size(SEQ)
    rows, channels = query_rows.shape
    spans = span_order.shape[0]
    span_rows = rows * devices // spans
    per_device = rows // span_rows
    taps = filters.shape[1]
    groups = filters.shape[0]
    group_size = channels // groups
    halo = -(-(taps - 1) // span_rows)
    lead = halo * span_rows
    window = lead + span_rows

    mixed = times_rounded(key_rows, value_rows)
    gated = times_rounded(grad_rows, query_rows)
    across = lax.all_gather(jnp.stack([mixed, gated]), CHIPS, axis=0, tiled=False)
    gathered = lax.all_gather(across, CORE, axis=0, tiled=False)
    cores = lax.axis_size(CORE)
    chips = devices // cores
    gathered = gathered.reshape(cores, chips, 2, per_device, span_rows, channels)
    mixed_blocks = gathered[:, :, 0].reshape(spans, span_rows, channels)
    gated_blocks = gathered[:, :, 1].reshape(spans, span_rows, channels)

    slot_of = jnp.zeros((spans,), jnp.int32).at[span_order].set(jnp.arange(spans, dtype=jnp.int32))
    mine = lax.dynamic_slice_in_dim(span_order, device * per_device, per_device)
    step = jnp.arange(halo, dtype=jnp.int32)
    before = mine[:, None] - halo + step[None, :]
    after = mine[:, None] + 1 + step[None, :]

    def pick(blocks, wanted):
        valid = (wanted >= 0) & (wanted < spans)
        slots = slot_of[jnp.clip(wanted, 0, spans - 1)].reshape(-1)
        holder = slots // per_device
        slots = ((holder % cores) * chips + holder // cores) * per_device + slots % per_device
        taken = jnp.take(blocks, slots, axis=0).reshape(per_device, halo, span_rows, channels)
        return jnp.where(valid[:, :, None, None], taken, jnp.zeros_like(taken))

    own_mixed = mixed.reshape(per_device, span_rows, channels)
    own_gated = gated.reshape(per_device, span_rows, channels)
    mixed_window = jnp.concatenate(
        [pick(mixed_blocks, before).reshape(per_device, lead, channels), own_mixed], axis=1
    )
    gated_window = jnp.concatenate(
        [own_gated, pick(gated_blocks, after).reshape(per_device, lead, channels)], axis=1
    )
    mixed_window = mixed_window.reshape(per_device, window, groups, group_size)
    gated_window = gated_window.reshape(per_device, window, groups, group_size)

    select_fwd = band_select(taps, span_rows, window, lead)
    fwd_band = jnp.einsum(
        "gj,jaw->gaw", filters, select_fwd, preferred_element_type=jnp.float32
    ).astype(jnp.bfloat16)
    bwd_band = jnp.einsum(
        "gj,jau->gau", filters, _bwd_select(taps, span_rows, window),
        preferred_element_type=jnp.float32,
    ).astype(jnp.bfloat16)

    conv = jnp.einsum("gaw,swgc->sagc", fwd_band, mixed_window, preferred_element_type=jnp.float32)
    convolved = conv.reshape(rows, channels).astype(jnp.bfloat16)
    adjoint = jnp.einsum("gau,sugc->sagc", bwd_band, gated_window, preferred_element_type=jnp.float32)
    dmixed = adjoint.reshape(rows, channels).astype(jnp.bfloat16)

    own_gated_g = own_gated.reshape(per_device, span_rows, groups, group_size)
    corr = jnp.einsum(
        "sagc,swgc->gaw", own_gated_g, mixed_window, preferred_element_type=jnp.float32
    )
    partial_grad = jnp.einsum(
        "gaw,jaw->gj", corr, select_fwd.astype(jnp.float32), precision=lax.Precision.HIGHEST
    )
    total_grad = partial_grad
    for axis in SEQ[::-1]:
        total_grad = lax.psum(total_grad, axis)
    squares = jnp.sum(total_grad * total_grad)
    for axis in CHAN[::-1]:
        squares = lax.psum(squares, axis)
    limit = math.sqrt(groups * lax.axis_size(CHAN) * taps)
    factor = jnp.minimum(1.0, limit / jnp.sqrt(squares + 1e-06))
    filter_grad = factor * total_grad

    gated_out = times_rounded(query_rows, convolved)
    grad_query = times_rounded(grad_rows, convolved)
    grad_key = times_rounded(dmixed, value_rows)
    grad_value = times_rounded(dmixed, key_rows)
    return (gated_out, grad_query, grad_key, grad_value, filter_grad)


def _bwd_select(taps, out_rows, window):
    j = lax.broadcasted_iota(jnp.int32, (taps, out_rows, window), 0)
    a = lax.broadcasted_iota(jnp.int32, (taps, out_rows, window), 1)
    u = lax.broadcasted_iota(jnp.int32, (taps, out_rows, window), 2)
    return (u == a + j).astype(jnp.bfloat16)


SEQ = ("zh", "y", "core")
CHAN = ("x", "zl")
CHIPS = ("zh", "y")
CORE = "core"


def solution(mesh):
    seq_size, chan_size = mesh.devices.shape
    split = mesh.devices.reshape(2, seq_size // 4, 2, chan_size // 2, 2)
    fine = jax.sharding.Mesh(split, SEQ + CHAN)
    rows = P(SEQ, CHAN)
    return jax.shard_map(
        shards,
        mesh=fine,
        in_specs=(rows, rows, rows, rows, P(CHAN, None), P()),
        out_specs=(rows, rows, rows, rows, P(CHAN, None)),
        check_vma=False,
    )
```

```python
import math

import jax
import jax.numpy as jnp
from jax import lax
from jax.sharding import PartitionSpec as P


def times_rounded(left, right):
    return (left.astype(jnp.float32) * right.astype(jnp.float32)).astype(jnp.bfloat16)


def butterfly_sum(value, axis):
    size = lax.axis_size(axis)
    bit = 1
    while bit < size:
        pairs = [(i, i ^ bit) for i in range(size)]
        value = value + lax.ppermute(value, axis, pairs)
        bit *= 2
    return value


def band_select(taps, out_rows, window, lead):
    j = lax.broadcasted_iota(jnp.int32, (taps, out_rows, window), 0)
    a = lax.broadcasted_iota(jnp.int32, (taps, out_rows, window), 1)
    w = lax.broadcasted_iota(jnp.int32, (taps, out_rows, window), 2)
    return (w == lead + a - j).astype(jnp.bfloat16)


def shards(query_rows, key_rows, value_rows, grad_rows, filters, span_order):
    device = lax.axis_index("seq")
    devices = lax.axis_size("seq")
    rows, channels = query_rows.shape
    spans = span_order.shape[0]
    span_rows = rows * devices // spans
    per_device = rows // span_rows
    taps = filters.shape[1]
    groups = filters.shape[0]
    group_size = channels // groups
    halo = -(-(taps - 1) // span_rows)
    lead = halo * span_rows
    window = lead + span_rows

    mixed = times_rounded(key_rows, value_rows)
    gated = times_rounded(grad_rows, query_rows)
    mixed_blocks = lax.all_gather(mixed, "seq", axis=0, tiled=True).reshape(spans, span_rows, channels)
    gated_blocks = lax.all_gather(gated, "seq", axis=0, tiled=True).reshape(spans, span_rows, channels)

    slot_of = jnp.zeros((spans,), jnp.int32).at[span_order].set(jnp.arange(spans, dtype=jnp.int32))
    mine = lax.dynamic_slice_in_dim(span_order, device * per_device, per_device)
    step = jnp.arange(halo, dtype=jnp.int32)
    before = mine[:, None] - halo + step[None, :]
    after = mine[:, None] + 1 + step[None, :]

    def pick(blocks, wanted):
        valid = (wanted >= 0) & (wanted < spans)
        slots = slot_of[jnp.clip(wanted, 0, spans - 1)].reshape(-1)
        taken = jnp.take(blocks, slots, axis=0).reshape(per_device, halo, span_rows, channels)
        return jnp.where(valid[:, :, None, None], taken, jnp.zeros_like(taken))

    own_mixed = mixed.reshape(per_device, span_rows, channels)
    own_gated = gated.reshape(per_device, span_rows, channels)
    mixed_window = jnp.concatenate(
        [pick(mixed_blocks, before).reshape(per_device, lead, channels), own_mixed], axis=1
    )
    gated_window = jnp.concatenate(
        [own_gated, pick(gated_blocks, after).reshape(per_device, lead, channels)], axis=1
    )
    mixed_window = mixed_window.reshape(per_device, window, groups, group_size)
    gated_window = gated_window.reshape(per_device, window, groups, group_size)

    select_fwd = band_select(taps, span_rows, window, lead)
    fwd_band = jnp.einsum(
        "gj,jaw->gaw", filters, select_fwd, preferred_element_type=jnp.float32
    ).astype(jnp.bfloat16)
    bwd_band = jnp.einsum(
        "gj,jau->gau", filters, _bwd_select(taps, span_rows, window),
        preferred_element_type=jnp.float32,
    ).astype(jnp.bfloat16)

    conv = jnp.einsum("gaw,swgc->sagc", fwd_band, mixed_window, preferred_element_type=jnp.float32)
    convolved = conv.reshape(rows, channels).astype(jnp.bfloat16)
    adjoint = jnp.einsum("gau,sugc->sagc", bwd_band, gated_window, preferred_element_type=jnp.float32)
    dmixed = adjoint.reshape(rows, channels).astype(jnp.bfloat16)

    own_gated_g = own_gated.reshape(per_device, span_rows, groups, group_size)
    corr = jnp.einsum(
        "sagc,swgc->gaw", own_gated_g, mixed_window, preferred_element_type=jnp.float32
    )
    partial_grad = jnp.einsum(
        "gaw,jaw->gj", corr, select_fwd.astype(jnp.float32), precision=lax.Precision.HIGHEST
    )
    total_grad = butterfly_sum(partial_grad, "seq")
    squares = butterfly_sum(jnp.sum(total_grad * total_grad), "chan")
    limit = math.sqrt(groups * lax.axis_size("chan") * taps)
    factor = jnp.minimum(1.0, limit / jnp.sqrt(squares + 1e-06))
    filter_grad = factor * total_grad

    gated_out = times_rounded(query_rows, convolved)
    grad_query = times_rounded(grad_rows, convolved)
    grad_key = times_rounded(dmixed, value_rows)
    grad_value = times_rounded(dmixed, key_rows)
    return (gated_out, grad_query, grad_key, grad_value, filter_grad)


def _bwd_select(taps, out_rows, window):
    j = lax.broadcasted_iota(jnp.int32, (taps, out_rows, window), 0)
    a = lax.broadcasted_iota(jnp.int32, (taps, out_rows, window), 1)
    u = lax.broadcasted_iota(jnp.int32, (taps, out_rows, window), 2)
    return (u == a + j).astype(jnp.bfloat16)


def solution(mesh):
    return jax.shard_map(
        shards,
        mesh=mesh,
        in_specs=(
            P("seq", "chan"),
            P("seq", "chan"),
            P("seq", "chan"),
            P("seq", "chan"),
            P("chan", None),
            P(),
        ),
        out_specs=(
            P("seq", "chan"),
            P("seq", "chan"),
            P("seq", "chan"),
            P("seq", "chan"),
            P("chan", None),
        ),
        check_vma=False,
    )
```

```python
import math

import jax
import jax.numpy as jnp
from jax import lax
from jax.sharding import PartitionSpec as P


def times_rounded(left, right):
    return (left.astype(jnp.float32) * right.astype(jnp.float32)).astype(jnp.bfloat16)


def butterfly_sum(value, axis):
    size = lax.axis_size(axis)
    bit = 1
    while bit < size:
        pairs = [(i, i ^ bit) for i in range(size)]
        value = value + lax.ppermute(value, axis, pairs)
        bit *= 2
    return value


def band_select(taps, out_rows, window, lead):
    j = lax.broadcasted_iota(jnp.int32, (taps, out_rows, window), 0)
    a = lax.broadcasted_iota(jnp.int32, (taps, out_rows, window), 1)
    w = lax.broadcasted_iota(jnp.int32, (taps, out_rows, window), 2)
    return (w == lead + a - j).astype(jnp.bfloat16)


def shards(query_rows, key_rows, value_rows, grad_rows, filters, span_order):
    device = lax.axis_index("seq")
    devices = lax.axis_size("seq")
    rows, channels = query_rows.shape
    spans = span_order.shape[0]
    span_rows = rows * devices // spans
    per_device = rows // span_rows
    taps = filters.shape[1]
    groups = filters.shape[0]
    group_size = channels // groups
    halo = -(-(taps - 1) // span_rows)
    lead = halo * span_rows
    window = lead + span_rows

    mixed = times_rounded(key_rows, value_rows)
    gated = times_rounded(grad_rows, query_rows)
    gathered = lax.all_gather(jnp.stack([mixed, gated]), "seq", axis=0, tiled=False)
    mixed_blocks = gathered[:, 0].reshape(spans, span_rows, channels)
    gated_blocks = gathered[:, 1].reshape(spans, span_rows, channels)

    slot_of = jnp.zeros((spans,), jnp.int32).at[span_order].set(jnp.arange(spans, dtype=jnp.int32))
    mine = lax.dynamic_slice_in_dim(span_order, device * per_device, per_device)
    step = jnp.arange(halo, dtype=jnp.int32)
    before = mine[:, None] - halo + step[None, :]
    after = mine[:, None] + 1 + step[None, :]

    def pick(blocks, wanted):
        valid = (wanted >= 0) & (wanted < spans)
        slots = slot_of[jnp.clip(wanted, 0, spans - 1)].reshape(-1)
        taken = jnp.take(blocks, slots, axis=0).reshape(per_device, halo, span_rows, channels)
        return jnp.where(valid[:, :, None, None], taken, jnp.zeros_like(taken))

    own_mixed = mixed.reshape(per_device, span_rows, channels)
    own_gated = gated.reshape(per_device, span_rows, channels)
    mixed_window = jnp.concatenate(
        [pick(mixed_blocks, before).reshape(per_device, lead, channels), own_mixed], axis=1
    )
    gated_window = jnp.concatenate(
        [own_gated, pick(gated_blocks, after).reshape(per_device, lead, channels)], axis=1
    )
    mixed_window = mixed_window.reshape(per_device, window, groups, group_size)
    gated_window = gated_window.reshape(per_device, window, groups, group_size)

    select_fwd = band_select(taps, span_rows, window, lead)
    fwd_band = jnp.einsum(
        "gj,jaw->gaw", filters, select_fwd, preferred_element_type=jnp.float32
    ).astype(jnp.bfloat16)
    bwd_band = jnp.einsum(
        "gj,jau->gau", filters, _bwd_select(taps, span_rows, window),
        preferred_element_type=jnp.float32,
    ).astype(jnp.bfloat16)

    conv = jnp.einsum("gaw,swgc->sagc", fwd_band, mixed_window, preferred_element_type=jnp.float32)
    convolved = conv.reshape(rows, channels).astype(jnp.bfloat16)
    adjoint = jnp.einsum("gau,sugc->sagc", bwd_band, gated_window, preferred_element_type=jnp.float32)
    dmixed = adjoint.reshape(rows, channels).astype(jnp.bfloat16)

    own_gated_g = own_gated.reshape(per_device, span_rows, groups, group_size)
    corr = jnp.einsum(
        "sagc,swgc->gaw", own_gated_g, mixed_window, preferred_element_type=jnp.float32
    )
    partial_grad = jnp.einsum(
        "gaw,jaw->gj", corr, select_fwd.astype(jnp.float32), precision=lax.Precision.HIGHEST
    )
    total_grad = butterfly_sum(partial_grad, "seq")
    squares = butterfly_sum(jnp.sum(total_grad * total_grad), "chan")
    limit = math.sqrt(groups * lax.axis_size("chan") * taps)
    factor = jnp.minimum(1.0, limit / jnp.sqrt(squares + 1e-06))
    filter_grad = factor * total_grad

    gated_out = times_rounded(query_rows, convolved)
    grad_query = times_rounded(grad_rows, convolved)
    grad_key = times_rounded(dmixed, value_rows)
    grad_value = times_rounded(dmixed, key_rows)
    return (gated_out, grad_query, grad_key, grad_value, filter_grad)


def _bwd_select(taps, out_rows, window):
    j = lax.broadcasted_iota(jnp.int32, (taps, out_rows, window), 0)
    a = lax.broadcasted_iota(jnp.int32, (taps, out_rows, window), 1)
    u = lax.broadcasted_iota(jnp.int32, (taps, out_rows, window), 2)
    return (u == a + j).astype(jnp.bfloat16)


def solution(mesh):
    return jax.shard_map(
        shards,
        mesh=mesh,
        in_specs=(
            P("seq", "chan"),
            P("seq", "chan"),
            P("seq", "chan"),
            P("seq", "chan"),
            P("chan", None),
            P(),
        ),
        out_specs=(
            P("seq", "chan"),
            P("seq", "chan"),
            P("seq", "chan"),
            P("seq", "chan"),
            P("chan", None),
        ),
        check_vma=False,
    )
```

```python
import math

import jax
import jax.numpy as jnp
from jax import lax
from jax.sharding import PartitionSpec as P


def times_rounded(left, right):
    return (left.astype(jnp.float32) * right.astype(jnp.float32)).astype(jnp.bfloat16)


def exchange_sum(value, axis):
    size = lax.axis_size(axis)
    me = lax.axis_index(axis)
    got = [value]
    for shift in range(1, size):
        pairs = [(i, (i + shift) % size) for i in range(size)]
        got.append(lax.ppermute(value, axis, pairs))
    stacked = jnp.stack(got)
    arranged = jnp.take(stacked, (me - jnp.arange(size)) % size, axis=0)
    return jnp.sum(arranged, axis=0)


def band_select(taps, out_rows, window, lead):
    j = lax.broadcasted_iota(jnp.int32, (taps, out_rows, window), 0)
    a = lax.broadcasted_iota(jnp.int32, (taps, out_rows, window), 1)
    w = lax.broadcasted_iota(jnp.int32, (taps, out_rows, window), 2)
    return (w == lead + a - j).astype(jnp.bfloat16)


def shards(query_rows, key_rows, value_rows, grad_rows, filters, span_order):
    device = lax.axis_index("seq")
    devices = lax.axis_size("seq")
    rows, channels = query_rows.shape
    spans = span_order.shape[0]
    span_rows = rows * devices // spans
    per_device = rows // span_rows
    taps = filters.shape[1]
    groups = filters.shape[0]
    group_size = channels // groups
    halo = -(-(taps - 1) // span_rows)
    lead = halo * span_rows
    window = lead + span_rows

    mixed = times_rounded(key_rows, value_rows)
    gated = times_rounded(grad_rows, query_rows)
    gathered = lax.all_gather(jnp.stack([mixed, gated]), "seq", axis=0, tiled=False)
    blocks = gathered.reshape(devices * 2 * per_device, span_rows, channels)

    slot_of = jnp.zeros((spans,), jnp.int32).at[span_order].set(jnp.arange(spans, dtype=jnp.int32))
    mine = lax.dynamic_slice_in_dim(span_order, device * per_device, per_device)
    step = jnp.arange(halo, dtype=jnp.int32)
    before = mine[:, None] - halo + step[None, :]
    after = mine[:, None] + 1 + step[None, :]

    def pick(which, wanted):
        valid = (wanted >= 0) & (wanted < spans)
        slots = slot_of[jnp.clip(wanted, 0, spans - 1)].reshape(-1)
        slots = ((slots // per_device) * 2 + which) * per_device + slots % per_device
        taken = jnp.take(blocks, slots, axis=0).reshape(per_device, halo, span_rows, channels)
        return jnp.where(valid[:, :, None, None], taken, jnp.zeros_like(taken))

    own_mixed = mixed.reshape(per_device, span_rows, channels)
    own_gated = gated.reshape(per_device, span_rows, channels)
    mixed_window = jnp.concatenate(
        [pick(0, before).reshape(per_device, lead, channels), own_mixed], axis=1
    )
    gated_window = jnp.concatenate(
        [own_gated, pick(1, after).reshape(per_device, lead, channels)], axis=1
    )
    mixed_window = mixed_window.reshape(per_device, window, groups, group_size)
    gated_window = gated_window.reshape(per_device, window, groups, group_size)

    select_fwd = band_select(taps, span_rows, window, lead)
    fwd_band = jnp.einsum(
        "gj,jaw->gaw", filters, select_fwd, preferred_element_type=jnp.float32
    ).astype(jnp.bfloat16)
    bwd_band = jnp.einsum(
        "gj,jau->gau", filters, _bwd_select(taps, span_rows, window),
        preferred_element_type=jnp.float32,
    ).astype(jnp.bfloat16)

    conv = jnp.einsum("gaw,swgc->sagc", fwd_band, mixed_window, preferred_element_type=jnp.float32)
    convolved = conv.reshape(rows, channels).astype(jnp.bfloat16)
    adjoint = jnp.einsum("gau,sugc->sagc", bwd_band, gated_window, preferred_element_type=jnp.float32)
    dmixed = adjoint.reshape(rows, channels).astype(jnp.bfloat16)

    own_gated_g = own_gated.reshape(per_device, span_rows, groups, group_size)
    corr = jnp.einsum(
        "sagc,swgc->gaw", own_gated_g, mixed_window, preferred_element_type=jnp.float32
    )
    partial_grad = jnp.einsum(
        "gaw,jaw->gj", corr, select_fwd.astype(jnp.float32), precision=lax.Precision.HIGHEST
    )
    total_grad = exchange_sum(partial_grad, "seq")
    squares = exchange_sum(jnp.sum(total_grad * total_grad), "chan")
    limit = math.sqrt(groups * lax.axis_size("chan") * taps)
    factor = jnp.minimum(1.0, limit / jnp.sqrt(squares + 1e-06))
    filter_grad = factor * total_grad

    gated_out = times_rounded(query_rows, convolved)
    grad_query = times_rounded(grad_rows, convolved)
    grad_key = times_rounded(dmixed, value_rows)
    grad_value = times_rounded(dmixed, key_rows)
    return (gated_out, grad_query, grad_key, grad_value, filter_grad)


def _bwd_select(taps, out_rows, window):
    j = lax.broadcasted_iota(jnp.int32, (taps, out_rows, window), 0)
    a = lax.broadcasted_iota(jnp.int32, (taps, out_rows, window), 1)
    u = lax.broadcasted_iota(jnp.int32, (taps, out_rows, window), 2)
    return (u == a + j).astype(jnp.bfloat16)


def solution(mesh):
    return jax.shard_map(
        shards,
        mesh=mesh,
        in_specs=(
            P("seq", "chan"),
            P("seq", "chan"),
            P("seq", "chan"),
            P("seq", "chan"),
            P("chan", None),
            P(),
        ),
        out_specs=(
            P("seq", "chan"),
            P("seq", "chan"),
            P("seq", "chan"),
            P("seq", "chan"),
            P("chan", None),
        ),
        check_vma=False,
    )
```

```python
import math

import jax
import jax.numpy as jnp
from jax import lax
from jax.sharding import PartitionSpec as P


def times_rounded(left, right):
    return (left.astype(jnp.float32) * right.astype(jnp.float32)).astype(jnp.bfloat16)


def butterfly_sum(value, axis):
    size = lax.axis_size(axis)
    bit = 1
    while bit < size:
        pairs = [(i, i ^ bit) for i in range(size)]
        value = value + lax.ppermute(value, axis, pairs)
        bit *= 2
    return value


def band_select(taps, out_rows, window, lead):
    j = lax.broadcasted_iota(jnp.int32, (taps, out_rows, window), 0)
    a = lax.broadcasted_iota(jnp.int32, (taps, out_rows, window), 1)
    w = lax.broadcasted_iota(jnp.int32, (taps, out_rows, window), 2)
    return (w == lead + a - j).astype(jnp.bfloat16)


def shards(query_rows, key_rows, value_rows, grad_rows, filters, span_order):
    device = lax.axis_index("seq")
    devices = lax.axis_size("seq")
    rows, channels = query_rows.shape
    spans = span_order.shape[0]
    span_rows = rows * devices // spans
    per_device = rows // span_rows
    taps = filters.shape[1]
    groups = filters.shape[0]
    group_size = channels // groups
    halo = -(-(taps - 1) // span_rows)
    lead = halo * span_rows
    window = lead + span_rows

    mixed = times_rounded(key_rows, value_rows)
    gated = times_rounded(grad_rows, query_rows)
    gathered = lax.all_gather(jnp.stack([mixed, gated]), "seq", axis=0, tiled=False)
    blocks = gathered.reshape(devices * 2 * per_device, span_rows, channels)

    slot_of = jnp.zeros((spans,), jnp.int32).at[span_order].set(jnp.arange(spans, dtype=jnp.int32))
    mine = lax.dynamic_slice_in_dim(span_order, device * per_device, per_device)
    step = jnp.arange(halo, dtype=jnp.int32)
    before = mine[:, None] - halo + step[None, :]
    after = mine[:, None] + 1 + step[None, :]

    def pick(which, wanted):
        valid = (wanted >= 0) & (wanted < spans)
        slots = slot_of[jnp.clip(wanted, 0, spans - 1)].reshape(-1)
        slots = ((slots // per_device) * 2 + which) * per_device + slots % per_device
        taken = jnp.take(blocks, slots, axis=0).reshape(per_device, halo, span_rows, channels)
        return jnp.where(valid[:, :, None, None], taken, jnp.zeros_like(taken))

    own_mixed = mixed.reshape(per_device, span_rows, channels)
    own_gated = gated.reshape(per_device, span_rows, channels)
    mixed_window = jnp.concatenate(
        [pick(0, before).reshape(per_device, lead, channels), own_mixed], axis=1
    )
    gated_window = jnp.concatenate(
        [own_gated, pick(1, after).reshape(per_device, lead, channels)], axis=1
    )
    mixed_window = mixed_window.reshape(per_device, window, groups, group_size)
    gated_window = gated_window.reshape(per_device, window, groups, group_size)

    select_fwd = band_select(taps, span_rows, window, lead)
    fwd_band = jnp.einsum(
        "gj,jaw->gaw", filters, select_fwd, preferred_element_type=jnp.float32
    ).astype(jnp.bfloat16)
    bwd_band = jnp.einsum(
        "gj,jau->gau", filters, _bwd_select(taps, span_rows, window),
        preferred_element_type=jnp.float32,
    ).astype(jnp.bfloat16)

    conv = jnp.einsum("gaw,swgc->sagc", fwd_band, mixed_window, preferred_element_type=jnp.float32)
    convolved = conv.reshape(rows, channels).astype(jnp.bfloat16)
    adjoint = jnp.einsum("gau,sugc->sagc", bwd_band, gated_window, preferred_element_type=jnp.float32)
    dmixed = adjoint.reshape(rows, channels).astype(jnp.bfloat16)

    own_gated_g = own_gated.reshape(per_device, span_rows, groups, group_size)
    corr = jnp.einsum(
        "sagc,swgc->gaw", own_gated_g, mixed_window, preferred_element_type=jnp.float32
    )
    partial_grad = jnp.einsum(
        "gaw,jaw->gj", corr, select_fwd.astype(jnp.float32), precision=lax.Precision.HIGHEST
    )
    total_grad = butterfly_sum(partial_grad, "seq")
    squares = butterfly_sum(jnp.sum(total_grad * total_grad), "chan")
    limit = math.sqrt(groups * lax.axis_size("chan") * taps)
    factor = jnp.minimum(1.0, limit / jnp.sqrt(squares + 1e-06))
    filter_grad = factor * total_grad

    gated_out = times_rounded(query_rows, convolved)
    grad_query = times_rounded(grad_rows, convolved)
    grad_key = times_rounded(dmixed, value_rows)
    grad_value = times_rounded(dmixed, key_rows)
    return (gated_out, grad_query, grad_key, grad_value, filter_grad)


def _bwd_select(taps, out_rows, window):
    j = lax.broadcasted_iota(jnp.int32, (taps, out_rows, window), 0)
    a = lax.broadcasted_iota(jnp.int32, (taps, out_rows, window), 1)
    u = lax.broadcasted_iota(jnp.int32, (taps, out_rows, window), 2)
    return (u == a + j).astype(jnp.bfloat16)


def solution(mesh):
    return jax.shard_map(
        shards,
        mesh=mesh,
        in_specs=(
            P("seq", "chan"),
            P("seq", "chan"),
            P("seq", "chan"),
            P("seq", "chan"),
            P("chan", None),
            P(),
        ),
        out_specs=(
            P("seq", "chan"),
            P("seq", "chan"),
            P("seq", "chan"),
            P("seq", "chan"),
            P("chan", None),
        ),
        check_vma=False,
    )
```

```python
import math

import jax
import jax.numpy as jnp
from jax import lax
from jax.sharding import PartitionSpec as P


def times_rounded(left, right):
    return (left.astype(jnp.float32) * right.astype(jnp.float32)).astype(jnp.bfloat16)


def butterfly_sum(value, axis):
    size = lax.axis_size(axis)

    def swap(v, mask):
        return lax.ppermute(v, axis, [(i, i ^ mask) for i in range(size)])

    bit = 1
    while bit < size:
        if bit * 4 <= size:
            value = (value + swap(value, bit)) + (swap(value, 2 * bit) + swap(value, 3 * bit))
            bit *= 4
        else:
            value = value + swap(value, bit)
            bit *= 2
    return value


def band_select(taps, out_rows, window, lead):
    j = lax.broadcasted_iota(jnp.int32, (taps, out_rows, window), 0)
    a = lax.broadcasted_iota(jnp.int32, (taps, out_rows, window), 1)
    w = lax.broadcasted_iota(jnp.int32, (taps, out_rows, window), 2)
    return (w == lead + a - j).astype(jnp.bfloat16)


def shards(query_rows, key_rows, value_rows, grad_rows, filters, span_order):
    device = lax.axis_index("seq")
    devices = lax.axis_size("seq")
    rows, channels = query_rows.shape
    spans = span_order.shape[0]
    span_rows = rows * devices // spans
    per_device = rows // span_rows
    taps = filters.shape[1]
    groups = filters.shape[0]
    group_size = channels // groups
    halo = -(-(taps - 1) // span_rows)
    lead = halo * span_rows
    window = lead + span_rows

    mixed = times_rounded(key_rows, value_rows)
    gated = times_rounded(grad_rows, query_rows)
    gathered = lax.all_gather(jnp.stack([mixed, gated]), "seq", axis=0, tiled=False)
    blocks = gathered.reshape(devices * 2 * per_device, span_rows, channels)

    slot_of = jnp.zeros((spans,), jnp.int32).at[span_order].set(jnp.arange(spans, dtype=jnp.int32))
    mine = lax.dynamic_slice_in_dim(span_order, device * per_device, per_device)
    step = jnp.arange(halo, dtype=jnp.int32)
    before = mine[:, None] - halo + step[None, :]
    after = mine[:, None] + 1 + step[None, :]

    def pick(which, wanted):
        valid = (wanted >= 0) & (wanted < spans)
        slots = slot_of[jnp.clip(wanted, 0, spans - 1)].reshape(-1)
        slots = ((slots // per_device) * 2 + which) * per_device + slots % per_device
        taken = jnp.take(blocks, slots, axis=0).reshape(per_device, halo, span_rows, channels)
        return jnp.where(valid[:, :, None, None], taken, jnp.zeros_like(taken))

    own_mixed = mixed.reshape(per_device, span_rows, channels)
    own_gated = gated.reshape(per_device, span_rows, channels)
    mixed_window = jnp.concatenate(
        [pick(0, before).reshape(per_device, lead, channels), own_mixed], axis=1
    )
    gated_window = jnp.concatenate(
        [own_gated, pick(1, after).reshape(per_device, lead, channels)], axis=1
    )
    mixed_window = mixed_window.reshape(per_device, window, groups, group_size)
    gated_window = gated_window.reshape(per_device, window, groups, group_size)

    select_fwd = band_select(taps, span_rows, window, lead)
    fwd_band = jnp.einsum(
        "gj,jaw->gaw", filters, select_fwd, preferred_element_type=jnp.float32
    ).astype(jnp.bfloat16)
    bwd_band = jnp.einsum(
        "gj,jau->gau", filters, _bwd_select(taps, span_rows, window),
        preferred_element_type=jnp.float32,
    ).astype(jnp.bfloat16)

    conv = jnp.einsum("gaw,swgc->sagc", fwd_band, mixed_window, preferred_element_type=jnp.float32)
    convolved = conv.reshape(rows, channels).astype(jnp.bfloat16)
    adjoint = jnp.einsum("gau,sugc->sagc", bwd_band, gated_window, preferred_element_type=jnp.float32)
    dmixed = adjoint.reshape(rows, channels).astype(jnp.bfloat16)

    own_gated_g = own_gated.reshape(per_device, span_rows, groups, group_size)
    corr = jnp.einsum(
        "sagc,swgc->gaw", own_gated_g, mixed_window, preferred_element_type=jnp.float32
    )
    partial_grad = jnp.einsum(
        "gaw,jaw->gj", corr, select_fwd.astype(jnp.float32), precision=lax.Precision.HIGHEST
    )
    total_grad = butterfly_sum(partial_grad, "seq")
    squares = butterfly_sum(jnp.sum(total_grad * total_grad), "chan")
    limit = math.sqrt(groups * lax.axis_size("chan") * taps)
    factor = jnp.minimum(1.0, limit / jnp.sqrt(squares + 1e-06))
    filter_grad = factor * total_grad

    gated_out = times_rounded(query_rows, convolved)
    grad_query = times_rounded(grad_rows, convolved)
    grad_key = times_rounded(dmixed, value_rows)
    grad_value = times_rounded(dmixed, key_rows)
    return (gated_out, grad_query, grad_key, grad_value, filter_grad)


def _bwd_select(taps, out_rows, window):
    j = lax.broadcasted_iota(jnp.int32, (taps, out_rows, window), 0)
    a = lax.broadcasted_iota(jnp.int32, (taps, out_rows, window), 1)
    u = lax.broadcasted_iota(jnp.int32, (taps, out_rows, window), 2)
    return (u == a + j).astype(jnp.bfloat16)


def solution(mesh):
    return jax.shard_map(
        shards,
        mesh=mesh,
        in_specs=(
            P("seq", "chan"),
            P("seq", "chan"),
            P("seq", "chan"),
            P("seq", "chan"),
            P("chan", None),
            P(),
        ),
        out_specs=(
            P("seq", "chan"),
            P("seq", "chan"),
            P("seq", "chan"),
            P("seq", "chan"),
            P("chan", None),
        ),
        check_vma=False,
    )
```

```python
import math

import jax
import jax.numpy as jnp
from jax import lax
from jax.sharding import PartitionSpec as P


def times_rounded(left, right):
    return (left.astype(jnp.float32) * right.astype(jnp.float32)).astype(jnp.bfloat16)


def butterfly_sum(value, axis):
    size = lax.axis_size(axis)

    def swap(v, mask):
        return lax.ppermute(v, axis, [(i, i ^ mask) for i in range(size)])

    bit = 1
    while bit < size:
        if bit * 4 <= size:
            value = (value + swap(value, bit)) + (swap(value, 2 * bit) + swap(value, 3 * bit))
            bit *= 4
        else:
            value = value + swap(value, bit)
            bit *= 2
    return value


def band_select(taps, out_rows, window, lead):
    j = lax.broadcasted_iota(jnp.int32, (taps, out_rows, window), 0)
    a = lax.broadcasted_iota(jnp.int32, (taps, out_rows, window), 1)
    w = lax.broadcasted_iota(jnp.int32, (taps, out_rows, window), 2)
    return (w == lead + a - j).astype(jnp.bfloat16)


def shards(query_rows, key_rows, value_rows, grad_rows, filters, span_order):
    device = lax.axis_index("seq")
    devices = lax.axis_size("seq")
    rows, channels = query_rows.shape
    spans = span_order.shape[0]
    span_rows = rows * devices // spans
    per_device = rows // span_rows
    taps = filters.shape[1]
    groups = filters.shape[0]
    group_size = channels // groups
    halo = -(-(taps - 1) // span_rows)
    lead = halo * span_rows
    window = lead + span_rows

    mixed = times_rounded(key_rows, value_rows)
    gated = times_rounded(grad_rows, query_rows)
    gathered = lax.all_gather(jnp.stack([mixed, gated]), "seq", axis=0, tiled=False)
    blocks = gathered.reshape(devices * 2 * per_device, span_rows, channels)

    slot_of = jnp.zeros((spans,), jnp.int32).at[span_order].set(jnp.arange(spans, dtype=jnp.int32))
    mine = lax.dynamic_slice_in_dim(span_order, device * per_device, per_device)
    step = jnp.arange(halo, dtype=jnp.int32)
    before = mine[:, None] - halo + step[None, :]
    after = mine[:, None] + 1 + step[None, :]

    def pick(which, wanted):
        valid = (wanted >= 0) & (wanted < spans)
        slots = slot_of[jnp.clip(wanted, 0, spans - 1)].reshape(-1)
        slots = ((slots // per_device) * 2 + which) * per_device + slots % per_device
        taken = jnp.take(blocks, slots, axis=0).reshape(per_device, halo, span_rows, channels)
        return jnp.where(valid[:, :, None, None], taken, jnp.zeros_like(taken))

    own_mixed = mixed.reshape(per_device, span_rows, groups, group_size)
    own_gated = gated.reshape(per_device, span_rows, groups, group_size)
    halo_mixed = pick(0, before).reshape(per_device, lead, groups, group_size)
    halo_gated = pick(1, after).reshape(per_device, lead, groups, group_size)

    select_fwd = band_select(taps, span_rows, window, lead)
    fwd_band = jnp.einsum(
        "gj,jaw->gaw", filters, select_fwd, preferred_element_type=jnp.float32
    ).astype(jnp.bfloat16)
    bwd_band = jnp.einsum(
        "gj,jau->gau", filters, _bwd_select(taps, span_rows, window),
        preferred_element_type=jnp.float32,
    ).astype(jnp.bfloat16)

    def band_apply(band, source):
        return jnp.einsum("gaw,swgc->sagc", band, source, preferred_element_type=jnp.float32)

    conv = band_apply(fwd_band[:, :, lead:], own_mixed) + band_apply(fwd_band[:, :, :lead], halo_mixed)
    convolved = conv.reshape(rows, channels).astype(jnp.bfloat16)
    adjoint = band_apply(bwd_band[:, :, :span_rows], own_gated) + band_apply(
        bwd_band[:, :, span_rows:], halo_gated
    )
    dmixed = adjoint.reshape(rows, channels).astype(jnp.bfloat16)

    def lag_sums(source, select):
        corr = jnp.einsum("sagc,swgc->gaw", own_gated, source, preferred_element_type=jnp.float32)
        return jnp.einsum(
            "gaw,jaw->gj", corr, select.astype(jnp.float32), precision=lax.Precision.HIGH
        )

    partial_grad = lag_sums(own_mixed, select_fwd[:, :, lead:]) + lag_sums(
        halo_mixed, select_fwd[:, :, :lead]
    )
    total_grad = butterfly_sum(partial_grad, "seq")
    squares = butterfly_sum(jnp.sum(total_grad * total_grad), "chan")
    limit = math.sqrt(groups * lax.axis_size("chan") * taps)
    factor = jnp.minimum(1.0, limit / jnp.sqrt(squares + 1e-06))
    filter_grad = factor * total_grad

    gated_out = times_rounded(query_rows, convolved)
    grad_query = times_rounded(grad_rows, convolved)
    grad_key = times_rounded(dmixed, value_rows)
    grad_value = times_rounded(dmixed, key_rows)
    return (gated_out, grad_query, grad_key, grad_value, filter_grad)


def _bwd_select(taps, out_rows, window):
    j = lax.broadcasted_iota(jnp.int32, (taps, out_rows, window), 0)
    a = lax.broadcasted_iota(jnp.int32, (taps, out_rows, window), 1)
    u = lax.broadcasted_iota(jnp.int32, (taps, out_rows, window), 2)
    return (u == a + j).astype(jnp.bfloat16)


def solution(mesh):
    return jax.shard_map(
        shards,
        mesh=mesh,
        in_specs=(
            P("seq", "chan"),
            P("seq", "chan"),
            P("seq", "chan"),
            P("seq", "chan"),
            P("chan", None),
            P(),
        ),
        out_specs=(
            P("seq", "chan"),
            P("seq", "chan"),
            P("seq", "chan"),
            P("seq", "chan"),
            P("chan", None),
        ),
        check_vma=False,
    )
```

```python
import math

import jax
import jax.numpy as jnp
from jax import lax
from jax.sharding import PartitionSpec as P


def times_rounded(left, right):
    return (left.astype(jnp.float32) * right.astype(jnp.float32)).astype(jnp.bfloat16)


def butterfly_sum(value, axis):
    size = lax.axis_size(axis)

    def swap(v, mask):
        return lax.ppermute(v, axis, [(i, i ^ mask) for i in range(size)])

    bit = 1
    while bit < size:
        if bit * 4 <= size:
            value = (value + swap(value, bit)) + (swap(value, 2 * bit) + swap(value, 3 * bit))
            bit *= 4
        else:
            value = value + swap(value, bit)
            bit *= 2
    return value


def band_select(taps, out_rows, window, lead):
    j = lax.broadcasted_iota(jnp.int32, (taps, out_rows, window), 0)
    a = lax.broadcasted_iota(jnp.int32, (taps, out_rows, window), 1)
    w = lax.broadcasted_iota(jnp.int32, (taps, out_rows, window), 2)
    return (w == lead + a - j).astype(jnp.bfloat16)


def shards(query_rows, key_rows, value_rows, grad_rows, filters, span_order):
    device = lax.axis_index("seq")
    devices = lax.axis_size("seq")
    rows, channels = query_rows.shape
    spans = span_order.shape[0]
    span_rows = rows * devices // spans
    per_device = rows // span_rows
    taps = filters.shape[1]
    groups = filters.shape[0]
    group_size = channels // groups
    halo = -(-(taps - 1) // span_rows)
    lead = halo * span_rows
    window = lead + span_rows

    mixed = times_rounded(key_rows, value_rows)
    gated = times_rounded(grad_rows, query_rows)
    gathered = lax.all_gather(jnp.stack([mixed, gated]), "seq", axis=0, tiled=False)
    blocks = gathered.reshape(devices * 2 * per_device, span_rows, channels)

    slot_of = jnp.zeros((spans,), jnp.int32).at[span_order].set(jnp.arange(spans, dtype=jnp.int32))
    mine = lax.dynamic_slice_in_dim(span_order, device * per_device, per_device)
    step = jnp.arange(halo, dtype=jnp.int32)
    before = mine[:, None] - halo + step[None, :]
    after = mine[:, None] + 1 + step[None, :]

    def pick(which, wanted):
        valid = (wanted >= 0) & (wanted < spans)
        slots = slot_of[jnp.clip(wanted, 0, spans - 1)].reshape(-1)
        slots = ((slots // per_device) * 2 + which) * per_device + slots % per_device
        taken = jnp.take(blocks, slots, axis=0).reshape(per_device, halo, span_rows, channels)
        return jnp.where(valid[:, :, None, None], taken, jnp.zeros_like(taken))

    own_mixed = mixed.reshape(per_device, span_rows, channels)
    own_gated = gated.reshape(per_device, span_rows, channels)
    mixed_window = jnp.concatenate(
        [pick(0, before).reshape(per_device, lead, channels), own_mixed], axis=1
    )
    gated_window = jnp.concatenate(
        [own_gated, pick(1, after).reshape(per_device, lead, channels)], axis=1
    )
    mixed_window = mixed_window.reshape(per_device, window, groups, group_size)
    gated_window = gated_window.reshape(per_device, window, groups, group_size)

    select_fwd = band_select(taps, span_rows, window, lead)
    fwd_band = jnp.einsum(
        "gj,jaw->gaw", filters, select_fwd, preferred_element_type=jnp.float32
    ).astype(jnp.bfloat16)
    bwd_band = jnp.einsum(
        "gj,jau->gau", filters, _bwd_select(taps, span_rows, window),
        preferred_element_type=jnp.float32,
    ).astype(jnp.bfloat16)

    conv = jnp.einsum("gaw,swgc->sagc", fwd_band, mixed_window, preferred_element_type=jnp.float32)
    convolved = conv.reshape(rows, channels).astype(jnp.bfloat16)
    adjoint = jnp.einsum("gau,sugc->sagc", bwd_band, gated_window, preferred_element_type=jnp.float32)
    dmixed = adjoint.reshape(rows, channels).astype(jnp.bfloat16)

    own_gated_g = own_gated.reshape(per_device, span_rows, groups, group_size)
    corr = jnp.einsum(
        "sagc,swgc->gaw", own_gated_g, mixed_window, preferred_element_type=jnp.float32
    )
    partial_grad = jnp.einsum(
        "gaw,jaw->gj", corr, select_fwd.astype(jnp.float32), precision=lax.Precision.HIGH
    )
    total_grad = butterfly_sum(partial_grad, "seq")
    squares = butterfly_sum(jnp.sum(total_grad * total_grad), "chan")
    limit = math.sqrt(groups * lax.axis_size("chan") * taps)
    factor = jnp.minimum(1.0, limit / jnp.sqrt(squares + 1e-06))
    filter_grad = factor * total_grad

    gated_out = times_rounded(query_rows, convolved)
    grad_query = times_rounded(grad_rows, convolved)
    grad_key = times_rounded(dmixed, value_rows)
    grad_value = times_rounded(dmixed, key_rows)
    return (gated_out, grad_query, grad_key, grad_value, filter_grad)


def _bwd_select(taps, out_rows, window):
    j = lax.broadcasted_iota(jnp.int32, (taps, out_rows, window), 0)
    a = lax.broadcasted_iota(jnp.int32, (taps, out_rows, window), 1)
    u = lax.broadcasted_iota(jnp.int32, (taps, out_rows, window), 2)
    return (u == a + j).astype(jnp.bfloat16)


def solution(mesh):
    return jax.shard_map(
        shards,
        mesh=mesh,
        in_specs=(
            P("seq", "chan"),
            P("seq", "chan"),
            P("seq", "chan"),
            P("seq", "chan"),
            P("chan", None),
            P(),
        ),
        out_specs=(
            P("seq", "chan"),
            P("seq", "chan"),
            P("seq", "chan"),
            P("seq", "chan"),
            P("chan", None),
        ),
        check_vma=False,
    )
```

```python
import math

import jax
import jax.numpy as jnp
from jax import lax
from jax.sharding import PartitionSpec as P


def times_rounded(left, right):
    return (left.astype(jnp.float32) * right.astype(jnp.float32)).astype(jnp.bfloat16)


def butterfly_sum(value, axis):
    size = lax.axis_size(axis)

    def swap(v, mask):
        return lax.ppermute(v, axis, [(i, i ^ mask) for i in range(size)])

    bit = 1
    while bit < size:
        if bit * 4 <= size:
            value = (value + swap(value, bit)) + (swap(value, 2 * bit) + swap(value, 3 * bit))
            bit *= 4
        else:
            value = value + swap(value, bit)
            bit *= 2
    return value


def band_select(taps, out_rows, window, lead):
    j = lax.broadcasted_iota(jnp.int32, (taps, out_rows, window), 0)
    a = lax.broadcasted_iota(jnp.int32, (taps, out_rows, window), 1)
    w = lax.broadcasted_iota(jnp.int32, (taps, out_rows, window), 2)
    return (w == lead + a - j).astype(jnp.bfloat16)


def shards(query_rows, key_rows, value_rows, grad_rows, filters, span_order):
    device = lax.axis_index("seq")
    devices = lax.axis_size("seq")
    rows, channels = query_rows.shape
    spans = span_order.shape[0]
    span_rows = rows * devices // spans
    per_device = rows // span_rows
    taps = filters.shape[1]
    groups = filters.shape[0]
    group_size = channels // groups
    halo = -(-(taps - 1) // span_rows)
    lead = halo * span_rows
    window = lead + span_rows

    mixed = times_rounded(key_rows, value_rows)
    gated = times_rounded(grad_rows, query_rows)
    gathered = lax.all_gather(jnp.stack([mixed, gated]), "seq", axis=0, tiled=False)
    blocks = gathered.reshape(devices * 2 * per_device, span_rows, channels)

    slot_of = jnp.zeros((spans,), jnp.int32).at[span_order].set(jnp.arange(spans, dtype=jnp.int32))
    mine = lax.dynamic_slice_in_dim(span_order, device * per_device, per_device)
    step = jnp.arange(halo, dtype=jnp.int32)
    before = mine[:, None] - halo + step[None, :]
    after = mine[:, None] + 1 + step[None, :]

    def pick(which, wanted):
        valid = (wanted >= 0) & (wanted < spans)
        slots = slot_of[jnp.clip(wanted, 0, spans - 1)].reshape(-1)
        slots = ((slots // per_device) * 2 + which) * per_device + slots % per_device
        taken = jnp.take(blocks, slots, axis=0).reshape(per_device, halo, span_rows, channels)
        return jnp.where(valid[:, :, None, None], taken, jnp.zeros_like(taken))

    own_mixed = mixed.reshape(per_device, span_rows, channels)
    own_gated = gated.reshape(per_device, span_rows, channels)
    mixed_window = jnp.concatenate(
        [pick(0, before).reshape(per_device, lead, channels), own_mixed], axis=1
    )
    gated_window = jnp.concatenate(
        [own_gated, pick(1, after).reshape(per_device, lead, channels)], axis=1
    )
    mixed_window = mixed_window.reshape(per_device, window, groups, group_size)
    gated_window = gated_window.reshape(per_device, window, groups, group_size)

    select_fwd = band_select(taps, span_rows, window, lead)
    fwd_band = jnp.einsum(
        "gj,jaw->gaw", filters, select_fwd, preferred_element_type=jnp.float32
    ).astype(jnp.bfloat16)
    bwd_band = jnp.einsum(
        "gj,jau->gau", filters, _bwd_select(taps, span_rows, window),
        preferred_element_type=jnp.float32,
    ).astype(jnp.bfloat16)

    conv = jnp.einsum("gaw,swgc->sagc", fwd_band, mixed_window, preferred_element_type=jnp.float32)
    convolved = conv.reshape(rows, channels).astype(jnp.bfloat16)
    adjoint = jnp.einsum("gau,sugc->sagc", bwd_band, gated_window, preferred_element_type=jnp.float32)
    dmixed = adjoint.reshape(rows, channels).astype(jnp.bfloat16)

    own_gated_g = own_gated.reshape(per_device, span_rows, groups, group_size)
    corr = jnp.einsum(
        "sagc,swgc->gaw", own_gated_g, mixed_window, preferred_element_type=jnp.float32
    )
    partial_grad = jnp.einsum(
        "gaw,jaw->gj", corr, select_fwd.astype(jnp.float32), precision=lax.Precision.HIGH
    )
    total_grad = butterfly_sum(partial_grad, "seq")
    squares = butterfly_sum(jnp.sum(total_grad * total_grad), "chan")
    limit = math.sqrt(groups * lax.axis_size("chan") * taps)
    factor = jnp.minimum(1.0, limit / jnp.sqrt(squares + 1e-06))
    filter_grad = factor * total_grad

    late_query, late_key, late_value, late_grad = lax.optimization_barrier(
        (query_rows, key_rows, value_rows, grad_rows)
    )
    gated_out = times_rounded(late_query, convolved)
    grad_query = times_rounded(late_grad, convolved)
    grad_key = times_rounded(dmixed, late_value)
    grad_value = times_rounded(dmixed, late_key)
    return (gated_out, grad_query, grad_key, grad_value, filter_grad)


def _bwd_select(taps, out_rows, window):
    j = lax.broadcasted_iota(jnp.int32, (taps, out_rows, window), 0)
    a = lax.broadcasted_iota(jnp.int32, (taps, out_rows, window), 1)
    u = lax.broadcasted_iota(jnp.int32, (taps, out_rows, window), 2)
    return (u == a + j).astype(jnp.bfloat16)


def solution(mesh):
    return jax.shard_map(
        shards,
        mesh=mesh,
        in_specs=(
            P("seq", "chan"),
            P("seq", "chan"),
            P("seq", "chan"),
            P("seq", "chan"),
            P("chan", None),
            P(),
        ),
        out_specs=(
            P("seq", "chan"),
            P("seq", "chan"),
            P("seq", "chan"),
            P("seq", "chan"),
            P("chan", None),
        ),
        check_vma=False,
    )
```

```python
import math

import jax
import jax.numpy as jnp
from jax import lax
from jax.sharding import PartitionSpec as P


def times_rounded(left, right):
    return (left.astype(jnp.float32) * right.astype(jnp.float32)).astype(jnp.bfloat16)


def swap(value, axis, mask):
    size = lax.axis_size(axis)
    return lax.ppermute(value, axis, [(i, i ^ mask) for i in range(size)])


def radix_round(value, axis, bit):
    if bit * 4 <= lax.axis_size(axis):
        return (value + swap(value, axis, bit)) + (swap(value, axis, 2 * bit) + swap(value, axis, 3 * bit)), bit * 4
    return value + swap(value, axis, bit), bit * 2


def butterfly_sum(value, axis):
    bit = 1
    while bit < lax.axis_size(axis):
        value, bit = radix_round(value, axis, bit)
    return value


def band_select(taps, out_rows, window, lead):
    j = lax.broadcasted_iota(jnp.int32, (taps, out_rows, window), 0)
    a = lax.broadcasted_iota(jnp.int32, (taps, out_rows, window), 1)
    w = lax.broadcasted_iota(jnp.int32, (taps, out_rows, window), 2)
    return (w == lead + a - j).astype(jnp.bfloat16)


def shards(query_rows, key_rows, value_rows, grad_rows, filters, span_order):
    device = lax.axis_index("seq")
    devices = lax.axis_size("seq")
    rows, channels = query_rows.shape
    spans = span_order.shape[0]
    span_rows = rows * devices // spans
    per_device = rows // span_rows
    taps = filters.shape[1]
    groups = filters.shape[0]
    group_size = channels // groups
    halo = -(-(taps - 1) // span_rows)
    lead = halo * span_rows
    window = lead + span_rows

    mixed = times_rounded(key_rows, value_rows)
    gated = times_rounded(grad_rows, query_rows)
    gathered = lax.all_gather(jnp.stack([mixed, gated]), "seq", axis=0, tiled=False)
    blocks = gathered.reshape(devices * 2 * per_device, span_rows, channels)

    slot_of = jnp.zeros((spans,), jnp.int32).at[span_order].set(jnp.arange(spans, dtype=jnp.int32))
    mine = lax.dynamic_slice_in_dim(span_order, device * per_device, per_device)
    step = jnp.arange(halo, dtype=jnp.int32)
    before = mine[:, None] - halo + step[None, :]
    after = mine[:, None] + 1 + step[None, :]

    def pick(blocks, which, wanted):
        valid = (wanted >= 0) & (wanted < spans)
        slots = slot_of[jnp.clip(wanted, 0, spans - 1)].reshape(-1)
        slots = ((slots // per_device) * 2 + which) * per_device + slots % per_device
        taken = jnp.take(blocks, slots, axis=0).reshape(per_device, halo, span_rows, channels)
        return jnp.where(valid[:, :, None, None], taken, jnp.zeros_like(taken))

    own_mixed = mixed.reshape(per_device, span_rows, channels)
    own_gated = gated.reshape(per_device, span_rows, channels)
    mixed_window = jnp.concatenate(
        [pick(blocks, 0, before).reshape(per_device, lead, channels), own_mixed], axis=1
    )
    mixed_window = mixed_window.reshape(per_device, window, groups, group_size)

    select_fwd = band_select(taps, span_rows, window, lead)
    fwd_band = jnp.einsum(
        "gj,jaw->gaw", filters, select_fwd, preferred_element_type=jnp.float32
    ).astype(jnp.bfloat16)
    bwd_band = jnp.einsum(
        "gj,jau->gau", filters, _bwd_select(taps, span_rows, window),
        preferred_element_type=jnp.float32,
    ).astype(jnp.bfloat16)

    conv = jnp.einsum("gaw,swgc->sagc", fwd_band, mixed_window, preferred_element_type=jnp.float32)
    convolved = conv.reshape(rows, channels).astype(jnp.bfloat16)
    own_gated_g = own_gated.reshape(per_device, span_rows, groups, group_size)
    corr = jnp.einsum(
        "sagc,swgc->gaw", own_gated_g, mixed_window, preferred_element_type=jnp.float32
    )
    partial_grad = jnp.einsum(
        "gaw,jaw->gj", corr, select_fwd.astype(jnp.float32), precision=lax.Precision.HIGH
    )
    total_grad, bit = radix_round(partial_grad, "seq", 1)
    total_grad, late_blocks = lax.optimization_barrier((total_grad, blocks))
    gated_window = jnp.concatenate(
        [own_gated, pick(late_blocks, 1, after).reshape(per_device, lead, channels)], axis=1
    ).reshape(per_device, window, groups, group_size)
    adjoint = jnp.einsum("gau,sugc->sagc", bwd_band, gated_window, preferred_element_type=jnp.float32)
    dmixed = adjoint.reshape(rows, channels).astype(jnp.bfloat16)
    while bit < devices:
        total_grad, bit = radix_round(total_grad, "seq", bit)
    total_grad, late_query, late_key, late_value, late_grad = lax.optimization_barrier(
        (total_grad, query_rows, key_rows, value_rows, grad_rows)
    )
    squares = butterfly_sum(jnp.sum(total_grad * total_grad), "chan")
    limit = math.sqrt(groups * lax.axis_size("chan") * taps)
    factor = jnp.minimum(1.0, limit / jnp.sqrt(squares + 1e-06))
    filter_grad = factor * total_grad

    gated_out = times_rounded(late_query, convolved)
    grad_query = times_rounded(late_grad, convolved)
    grad_key = times_rounded(dmixed, late_value)
    grad_value = times_rounded(dmixed, late_key)
    return (gated_out, grad_query, grad_key, grad_value, filter_grad)


def _bwd_select(taps, out_rows, window):
    j = lax.broadcasted_iota(jnp.int32, (taps, out_rows, window), 0)
    a = lax.broadcasted_iota(jnp.int32, (taps, out_rows, window), 1)
    u = lax.broadcasted_iota(jnp.int32, (taps, out_rows, window), 2)
    return (u == a + j).astype(jnp.bfloat16)


def solution(mesh):
    return jax.shard_map(
        shards,
        mesh=mesh,
        in_specs=(
            P("seq", "chan"),
            P("seq", "chan"),
            P("seq", "chan"),
            P("seq", "chan"),
            P("chan", None),
            P(),
        ),
        out_specs=(
            P("seq", "chan"),
            P("seq", "chan"),
            P("seq", "chan"),
            P("seq", "chan"),
            P("chan", None),
        ),
        check_vma=False,
    )
```

```python
import math

import jax
import jax.numpy as jnp
from jax import lax
from jax.sharding import PartitionSpec as P


def times_rounded(left, right):
    return (left.astype(jnp.float32) * right.astype(jnp.float32)).astype(jnp.bfloat16)


def swap(value, axis, mask):
    size = lax.axis_size(axis)
    return lax.ppermute(value, axis, [(i, i ^ mask) for i in range(size)])


def radix_round(value, axis, bit):
    if bit * 4 <= lax.axis_size(axis):
        return (value + swap(value, axis, bit)) + (swap(value, axis, 2 * bit) + swap(value, axis, 3 * bit)), bit * 4
    return value + swap(value, axis, bit), bit * 2


def butterfly_sum(value, axis):
    bit = 1
    while bit < lax.axis_size(axis):
        value, bit = radix_round(value, axis, bit)
    return value


def band_select(taps, out_rows, window, lead):
    j = lax.broadcasted_iota(jnp.int32, (taps, out_rows, window), 0)
    a = lax.broadcasted_iota(jnp.int32, (taps, out_rows, window), 1)
    w = lax.broadcasted_iota(jnp.int32, (taps, out_rows, window), 2)
    return (w == lead + a - j).astype(jnp.bfloat16)


def shards(query_rows, key_rows, value_rows, grad_rows, filters, span_order):
    device = lax.axis_index("seq")
    devices = lax.axis_size("seq")
    rows, channels = query_rows.shape
    spans = span_order.shape[0]
    span_rows = rows * devices // spans
    per_device = rows // span_rows
    taps = filters.shape[1]
    groups = filters.shape[0]
    group_size = channels // groups
    halo = -(-(taps - 1) // span_rows)
    lead = halo * span_rows
    window = lead + span_rows

    mixed = times_rounded(key_rows, value_rows)
    gated = times_rounded(grad_rows, query_rows)
    gathered = lax.all_gather(jnp.stack([mixed, gated]), "seq", axis=0, tiled=False)
    blocks = gathered.reshape(devices * 2 * per_device, span_rows, channels)

    slot_of = jnp.zeros((spans,), jnp.int32).at[span_order].set(jnp.arange(spans, dtype=jnp.int32))
    mine = lax.dynamic_slice_in_dim(span_order, device * per_device, per_device)
    step = jnp.arange(halo, dtype=jnp.int32)
    before = mine[:, None] - halo + step[None, :]
    after = mine[:, None] + 1 + step[None, :]

    def pick(blocks, which, wanted):
        valid = (wanted >= 0) & (wanted < spans)
        slots = slot_of[jnp.clip(wanted, 0, spans - 1)].reshape(-1)
        slots = ((slots // per_device) * 2 + which) * per_device + slots % per_device
        taken = jnp.take(blocks, slots, axis=0).reshape(per_device, halo, span_rows, channels)
        return jnp.where(valid[:, :, None, None], taken, jnp.zeros_like(taken))

    own_mixed = mixed.reshape(per_device, span_rows, channels)
    own_gated = gated.reshape(per_device, span_rows, channels)
    mixed_window = jnp.concatenate(
        [pick(blocks, 0, before).reshape(per_device, lead, channels), own_mixed], axis=1
    )
    mixed_window = mixed_window.reshape(per_device, window, groups, group_size)

    select_fwd = band_select(taps, span_rows, window, lead)
    fwd_band = jnp.einsum(
        "gj,jaw->gaw", filters, select_fwd, preferred_element_type=jnp.float32
    ).astype(jnp.bfloat16)
    bwd_band = jnp.einsum(
        "gj,jau->gau", filters, _bwd_select(taps, span_rows, window),
        preferred_element_type=jnp.float32,
    ).astype(jnp.bfloat16)

    conv = jnp.einsum("gaw,swgc->sagc", fwd_band, mixed_window, preferred_element_type=jnp.float32)
    convolved = conv.reshape(rows, channels).astype(jnp.bfloat16)
    own_gated_g = own_gated.reshape(per_device, span_rows, groups, group_size)
    corr = jnp.einsum(
        "sagc,swgc->gaw", own_gated_g, mixed_window, preferred_element_type=jnp.float32
    )
    partial_grad = jnp.einsum(
        "gaw,jaw->gj", corr, select_fwd.astype(jnp.float32), precision=lax.Precision.HIGH
    )
    partial_grad, late_blocks = lax.optimization_barrier((partial_grad, blocks))
    gated_window = jnp.concatenate(
        [own_gated, pick(late_blocks, 1, after).reshape(per_device, lead, channels)], axis=1
    ).reshape(per_device, window, groups, group_size)
    total_grad, bit = radix_round(partial_grad, "seq", 1)
    total_grad, gated_window = lax.optimization_barrier((total_grad, gated_window))
    adjoint = jnp.einsum("gau,sugc->sagc", bwd_band, gated_window, preferred_element_type=jnp.float32)
    dmixed = adjoint.reshape(rows, channels).astype(jnp.bfloat16)
    while bit < devices:
        total_grad, bit = radix_round(total_grad, "seq", bit)
    total_grad, late_query, late_key, late_value, late_grad = lax.optimization_barrier(
        (total_grad, query_rows, key_rows, value_rows, grad_rows)
    )
    squares = butterfly_sum(jnp.sum(total_grad * total_grad), "chan")
    limit = math.sqrt(groups * lax.axis_size("chan") * taps)
    factor = jnp.minimum(1.0, limit / jnp.sqrt(squares + 1e-06))
    filter_grad = factor * total_grad

    gated_out = times_rounded(late_query, convolved)
    grad_query = times_rounded(late_grad, convolved)
    grad_key = times_rounded(dmixed, late_value)
    grad_value = times_rounded(dmixed, late_key)
    return (gated_out, grad_query, grad_key, grad_value, filter_grad)


def _bwd_select(taps, out_rows, window):
    j = lax.broadcasted_iota(jnp.int32, (taps, out_rows, window), 0)
    a = lax.broadcasted_iota(jnp.int32, (taps, out_rows, window), 1)
    u = lax.broadcasted_iota(jnp.int32, (taps, out_rows, window), 2)
    return (u == a + j).astype(jnp.bfloat16)


def solution(mesh):
    return jax.shard_map(
        shards,
        mesh=mesh,
        in_specs=(
            P("seq", "chan"),
            P("seq", "chan"),
            P("seq", "chan"),
            P("seq", "chan"),
            P("chan", None),
            P(),
        ),
        out_specs=(
            P("seq", "chan"),
            P("seq", "chan"),
            P("seq", "chan"),
            P("seq", "chan"),
            P("chan", None),
        ),
        check_vma=False,
    )
```

```python
import math

import jax
import jax.numpy as jnp
from jax import lax
from jax.sharding import PartitionSpec as P


def times_rounded(left, right):
    return (left.astype(jnp.float32) * right.astype(jnp.float32)).astype(jnp.bfloat16)


def swap(value, axis, mask):
    size = lax.axis_size(axis)
    return lax.ppermute(value, axis, [(i, i ^ mask) for i in range(size)])


def radix_round(value, axis, low, high=None):
    if high is None:
        return value + swap(value, axis, 1 << low)
    one, two = 1 << low, 1 << high
    return (value + swap(value, axis, one)) + (swap(value, axis, two) + swap(value, axis, one | two))


def butterfly_sum(value, axis, rounds):
    for bits in rounds:
        value = radix_round(value, axis, *bits)
    return value


def band_select(taps, out_rows, window, lead):
    j = lax.broadcasted_iota(jnp.int32, (taps, out_rows, window), 0)
    a = lax.broadcasted_iota(jnp.int32, (taps, out_rows, window), 1)
    w = lax.broadcasted_iota(jnp.int32, (taps, out_rows, window), 2)
    return (w == lead + a - j).astype(jnp.bfloat16)


def shards(query_rows, key_rows, value_rows, grad_rows, filters, span_order):
    device = lax.axis_index("seq")
    devices = lax.axis_size("seq")
    rows, channels = query_rows.shape
    spans = span_order.shape[0]
    span_rows = rows * devices // spans
    per_device = rows // span_rows
    taps = filters.shape[1]
    groups = filters.shape[0]
    group_size = channels // groups
    halo = -(-(taps - 1) // span_rows)
    lead = halo * span_rows
    window = lead + span_rows

    mixed = times_rounded(key_rows, value_rows)
    gated = times_rounded(grad_rows, query_rows)
    gathered = lax.all_gather(jnp.stack([mixed, gated]), "seq", axis=0, tiled=False)
    blocks = gathered.reshape(devices * 2 * per_device, span_rows, channels)

    slot_of = jnp.zeros((spans,), jnp.int32).at[span_order].set(jnp.arange(spans, dtype=jnp.int32))
    mine = lax.dynamic_slice_in_dim(span_order, device * per_device, per_device)
    step = jnp.arange(halo, dtype=jnp.int32)
    before = mine[:, None] - halo + step[None, :]
    after = mine[:, None] + 1 + step[None, :]

    def pick(blocks, which, wanted):
        valid = (wanted >= 0) & (wanted < spans)
        slots = slot_of[jnp.clip(wanted, 0, spans - 1)].reshape(-1)
        slots = ((slots // per_device) * 2 + which) * per_device + slots % per_device
        taken = jnp.take(blocks, slots, axis=0).reshape(per_device, halo, span_rows, channels)
        return jnp.where(valid[:, :, None, None], taken, jnp.zeros_like(taken))

    own_mixed = mixed.reshape(per_device, span_rows, channels)
    own_gated = gated.reshape(per_device, span_rows, channels)
    mixed_window = jnp.concatenate(
        [pick(blocks, 0, before).reshape(per_device, lead, channels), own_mixed], axis=1
    )
    mixed_window = mixed_window.reshape(per_device, window, groups, group_size)

    select_fwd = band_select(taps, span_rows, window, lead)
    fwd_band = jnp.einsum(
        "gj,jaw->gaw", filters, select_fwd, preferred_element_type=jnp.float32
    ).astype(jnp.bfloat16)
    bwd_band = jnp.einsum(
        "gj,jau->gau", filters, _bwd_select(taps, span_rows, window),
        preferred_element_type=jnp.float32,
    ).astype(jnp.bfloat16)

    conv = jnp.einsum("gaw,swgc->sagc", fwd_band, mixed_window, preferred_element_type=jnp.float32)
    convolved = conv.reshape(rows, channels).astype(jnp.bfloat16)
    own_gated_g = own_gated.reshape(per_device, span_rows, groups, group_size)
    corr = jnp.einsum(
        "sagc,swgc->gaw", own_gated_g, mixed_window, preferred_element_type=jnp.float32
    )
    corr_high = corr.astype(jnp.bfloat16)
    corr_low = (corr - corr_high.astype(jnp.float32)).astype(jnp.bfloat16)
    partial_grad = jnp.einsum(
        "gaw,jaw->gj", corr_high, select_fwd, preferred_element_type=jnp.float32
    ) + jnp.einsum("gaw,jaw->gj", corr_low, select_fwd, preferred_element_type=jnp.float32)
    seq_rounds = ((0, 3), (1, 2))
    total_grad = radix_round(partial_grad, "seq", *seq_rounds[0])
    total_grad, late_blocks = lax.optimization_barrier((total_grad, blocks))
    gated_window = jnp.concatenate(
        [own_gated, pick(late_blocks, 1, after).reshape(per_device, lead, channels)], axis=1
    ).reshape(per_device, window, groups, group_size)
    adjoint = jnp.einsum("gau,sugc->sagc", bwd_band, gated_window, preferred_element_type=jnp.float32)
    dmixed = adjoint.reshape(rows, channels).astype(jnp.bfloat16)
    total_grad = butterfly_sum(total_grad, "seq", seq_rounds[1:])
    total_grad, late_query, late_key, late_value, late_grad = lax.optimization_barrier(
        (total_grad, query_rows, key_rows, value_rows, grad_rows)
    )
    squares = butterfly_sum(jnp.sum(total_grad * total_grad), "chan", ((1, 2), (0,)))
    limit = math.sqrt(groups * lax.axis_size("chan") * taps)
    factor = jnp.minimum(1.0, limit / jnp.sqrt(squares + 1e-06))
    filter_grad = factor * total_grad

    gated_out = times_rounded(late_query, convolved)
    grad_query = times_rounded(late_grad, convolved)
    grad_key = times_rounded(dmixed, late_value)
    grad_value = times_rounded(dmixed, late_key)
    return (gated_out, grad_query, grad_key, grad_value, filter_grad)


def _bwd_select(taps, out_rows, window):
    j = lax.broadcasted_iota(jnp.int32, (taps, out_rows, window), 0)
    a = lax.broadcasted_iota(jnp.int32, (taps, out_rows, window), 1)
    u = lax.broadcasted_iota(jnp.int32, (taps, out_rows, window), 2)
    return (u == a + j).astype(jnp.bfloat16)


def solution(mesh):
    return jax.shard_map(
        shards,
        mesh=mesh,
        in_specs=(
            P("seq", "chan"),
            P("seq", "chan"),
            P("seq", "chan"),
            P("seq", "chan"),
            P("chan", None),
            P(),
        ),
        out_specs=(
            P("seq", "chan"),
            P("seq", "chan"),
            P("seq", "chan"),
            P("seq", "chan"),
            P("chan", None),
        ),
        check_vma=False,
    )
```

```python
import math

import jax
import jax.numpy as jnp
from jax import lax
from jax.sharding import PartitionSpec as P


def times_rounded(left, right):
    return (left.astype(jnp.float32) * right.astype(jnp.float32)).astype(jnp.bfloat16)


def swap(value, axis, mask):
    size = lax.axis_size(axis)
    return lax.ppermute(value, axis, [(i, i ^ mask) for i in range(size)])


def radix_round(value, axis, low, high=None):
    if high is None:
        return value + swap(value, axis, 1 << low)
    one, two = 1 << low, 1 << high
    return (value + swap(value, axis, one)) + (swap(value, axis, two) + swap(value, axis, one | two))


def butterfly_sum(value, axis, rounds):
    for bits in rounds:
        value = radix_round(value, axis, *bits)
    return value


def band_select(taps, out_rows, window, lead):
    j = lax.broadcasted_iota(jnp.int32, (taps, out_rows, window), 0)
    a = lax.broadcasted_iota(jnp.int32, (taps, out_rows, window), 1)
    w = lax.broadcasted_iota(jnp.int32, (taps, out_rows, window), 2)
    return (w == lead + a - j).astype(jnp.bfloat16)


def shards(query_rows, key_rows, value_rows, grad_rows, filters, span_order):
    device = lax.axis_index("seq")
    devices = lax.axis_size("seq")
    rows, channels = query_rows.shape
    spans = span_order.shape[0]
    span_rows = rows * devices // spans
    per_device = rows // span_rows
    taps = filters.shape[1]
    groups = filters.shape[0]
    group_size = channels // groups
    halo = -(-(taps - 1) // span_rows)
    lead = halo * span_rows
    window = lead + span_rows

    mixed = times_rounded(key_rows, value_rows)
    gated = times_rounded(grad_rows, query_rows)
    gathered = lax.all_gather(jnp.stack([mixed, gated]), "seq", axis=0, tiled=False)
    blocks = gathered.reshape(devices * 2 * per_device, span_rows, channels)

    slot_of = jnp.zeros((spans,), jnp.int32).at[span_order].set(jnp.arange(spans, dtype=jnp.int32))
    mine = lax.dynamic_slice_in_dim(span_order, device * per_device, per_device)
    step = jnp.arange(halo, dtype=jnp.int32)
    before = mine[:, None] - halo + step[None, :]
    after = mine[:, None] + 1 + step[None, :]

    def pick(blocks, which, wanted):
        valid = (wanted >= 0) & (wanted < spans)
        slots = slot_of[jnp.clip(wanted, 0, spans - 1)].reshape(-1)
        slots = ((slots // per_device) * 2 + which) * per_device + slots % per_device
        taken = jnp.take(blocks, slots, axis=0).reshape(per_device, halo, span_rows, channels)
        return jnp.where(valid[:, :, None, None], taken, jnp.zeros_like(taken))

    own_mixed = mixed.reshape(per_device, span_rows, channels)
    own_gated = gated.reshape(per_device, span_rows, channels)
    mixed_window = jnp.concatenate(
        [pick(blocks, 0, before).reshape(per_device, lead, channels), own_mixed], axis=1
    )
    mixed_window = mixed_window.reshape(per_device, window, groups, group_size)

    select_fwd = band_select(taps, span_rows, window, lead)
    fwd_band = jnp.einsum(
        "gj,jaw->gaw", filters, select_fwd, preferred_element_type=jnp.float32
    ).astype(jnp.bfloat16)
    bwd_band = jnp.einsum(
        "gj,jau->gau", filters, _bwd_select(taps, span_rows, window),
        preferred_element_type=jnp.float32,
    ).astype(jnp.bfloat16)

    conv = jnp.einsum("gaw,swgc->sagc", fwd_band, mixed_window, preferred_element_type=jnp.float32)
    convolved = conv.reshape(rows, channels).astype(jnp.bfloat16)
    own_gated_g = own_gated.reshape(per_device, span_rows, groups, group_size)
    corr = jnp.einsum(
        "sagc,swgc->gaw", own_gated_g, mixed_window, preferred_element_type=jnp.float32
    )
    partial_grad = jnp.einsum(
        "gaw,jaw->gj", corr, select_fwd.astype(jnp.float32), precision=lax.Precision.HIGH
    )
    seq_rounds = ((0, 3), (1, 2))
    total_grad = radix_round(partial_grad, "seq", *seq_rounds[0])
    total_grad, late_blocks = lax.optimization_barrier((total_grad, blocks))
    gated_window = jnp.concatenate(
        [own_gated, pick(late_blocks, 1, after).reshape(per_device, lead, channels)], axis=1
    ).reshape(per_device, window, groups, group_size)
    total_grad = butterfly_sum(total_grad, "seq", seq_rounds[1:])
    total_grad, gated_window, late_query, late_key, late_value, late_grad = lax.optimization_barrier(
        (total_grad, gated_window, query_rows, key_rows, value_rows, grad_rows)
    )
    adjoint = jnp.einsum("gau,sugc->sagc", bwd_band, gated_window, preferred_element_type=jnp.float32)
    dmixed = adjoint.reshape(rows, channels).astype(jnp.bfloat16)
    squares = butterfly_sum(jnp.sum(total_grad * total_grad), "chan", ((1, 2), (0,)))
    limit = math.sqrt(groups * lax.axis_size("chan") * taps)
    factor = jnp.minimum(1.0, limit / jnp.sqrt(squares + 1e-06))
    filter_grad = factor * total_grad

    gated_out = times_rounded(late_query, convolved)
    grad_query = times_rounded(late_grad, convolved)
    grad_key = times_rounded(dmixed, late_value)
    grad_value = times_rounded(dmixed, late_key)
    return (gated_out, grad_query, grad_key, grad_value, filter_grad)


def _bwd_select(taps, out_rows, window):
    j = lax.broadcasted_iota(jnp.int32, (taps, out_rows, window), 0)
    a = lax.broadcasted_iota(jnp.int32, (taps, out_rows, window), 1)
    u = lax.broadcasted_iota(jnp.int32, (taps, out_rows, window), 2)
    return (u == a + j).astype(jnp.bfloat16)


def solution(mesh):
    return jax.shard_map(
        shards,
        mesh=mesh,
        in_specs=(
            P("seq", "chan"),
            P("seq", "chan"),
            P("seq", "chan"),
            P("seq", "chan"),
            P("chan", None),
            P(),
        ),
        out_specs=(
            P("seq", "chan"),
            P("seq", "chan"),
            P("seq", "chan"),
            P("seq", "chan"),
            P("chan", None),
        ),
        check_vma=False,
    )
```

```python
import math

import jax
import jax.numpy as jnp
from jax import lax
from jax.sharding import PartitionSpec as P


def times_rounded(left, right):
    return (left.astype(jnp.float32) * right.astype(jnp.float32)).astype(jnp.bfloat16)


def swap(value, axis, mask):
    size = lax.axis_size(axis)
    return lax.ppermute(value, axis, [(i, i ^ mask) for i in range(size)])


def radix_round(value, axis, low, high=None):
    if high is None:
        return value + swap(value, axis, 1 << low)
    one, two = 1 << low, 1 << high
    return (value + swap(value, axis, one)) + (swap(value, axis, two) + swap(value, axis, one | two))


def butterfly_sum(value, axis, rounds):
    for bits in rounds:
        value = radix_round(value, axis, *bits)
    return value


def band_select(taps, out_rows, window, lead):
    j = lax.broadcasted_iota(jnp.int32, (taps, out_rows, window), 0)
    a = lax.broadcasted_iota(jnp.int32, (taps, out_rows, window), 1)
    w = lax.broadcasted_iota(jnp.int32, (taps, out_rows, window), 2)
    return (w == lead + a - j).astype(jnp.bfloat16)


def shards(query_rows, key_rows, value_rows, grad_rows, filters, span_order):
    device = lax.axis_index("seq")
    devices = lax.axis_size("seq")
    rows, channels = query_rows.shape
    spans = span_order.shape[0]
    span_rows = rows * devices // spans
    per_device = rows // span_rows
    taps = filters.shape[1]
    groups = filters.shape[0]
    group_size = channels // groups
    halo = -(-(taps - 1) // span_rows)
    lead = halo * span_rows
    window = lead + span_rows

    mixed = times_rounded(key_rows, value_rows)
    gated = times_rounded(grad_rows, query_rows)
    gathered = lax.all_gather(jnp.stack([mixed, gated]), "seq", axis=0, tiled=False)
    blocks = gathered.reshape(devices * 2 * per_device, span_rows, channels)

    slot_of = jnp.zeros((spans,), jnp.int32).at[span_order].set(jnp.arange(spans, dtype=jnp.int32))
    mine = lax.dynamic_slice_in_dim(span_order, device * per_device, per_device)
    step = jnp.arange(halo, dtype=jnp.int32)
    before = mine[:, None] - halo + step[None, :]
    after = mine[:, None] + 1 + step[None, :]

    def pick(blocks, which, wanted):
        valid = (wanted >= 0) & (wanted < spans)
        slots = slot_of[jnp.clip(wanted, 0, spans - 1)].reshape(-1)
        slots = ((slots // per_device) * 2 + which) * per_device + slots % per_device
        taken = jnp.take(blocks, slots, axis=0).reshape(per_device, halo, span_rows, channels)
        return jnp.where(valid[:, :, None, None], taken, jnp.zeros_like(taken))

    own_mixed = mixed.reshape(per_device, span_rows, channels)
    own_gated = gated.reshape(per_device, span_rows, channels)
    mixed_window = jnp.concatenate(
        [pick(blocks, 0, before).reshape(per_device, lead, channels), own_mixed], axis=1
    )
    mixed_window = mixed_window.reshape(per_device, window, groups, group_size)

    select_fwd = band_select(taps, span_rows, window, lead)
    fwd_band = jnp.einsum(
        "gj,jaw->gaw", filters, select_fwd, preferred_element_type=jnp.float32
    ).astype(jnp.bfloat16)
    bwd_band = jnp.einsum(
        "gj,jau->gau", filters, _bwd_select(taps, span_rows, window),
        preferred_element_type=jnp.float32,
    ).astype(jnp.bfloat16)

    conv = jnp.einsum("gaw,swgc->sagc", fwd_band, mixed_window, preferred_element_type=jnp.float32)
    convolved = conv.reshape(rows, channels).astype(jnp.bfloat16)
    own_gated_g = own_gated.reshape(per_device, span_rows, groups, group_size)
    corr = jnp.einsum(
        "sagc,swgc->gaw", own_gated_g, mixed_window, preferred_element_type=jnp.float32
    )
    partial_grad = jnp.einsum(
        "gaw,jaw->gj", corr, select_fwd.astype(jnp.float32), precision=lax.Precision.HIGH
    )
    seq_rounds = ((0, 3), (1, 2))
    total_grad = radix_round(partial_grad, "seq", *seq_rounds[0])
    total_grad, late_blocks = lax.optimization_barrier((total_grad, blocks))
    gated_window = jnp.concatenate(
        [own_gated, pick(late_blocks, 1, after).reshape(per_device, lead, channels)], axis=1
    ).reshape(per_device, window, groups, group_size)
    total_grad = butterfly_sum(total_grad, "seq", seq_rounds[1:])
    total_grad, gated_window = lax.optimization_barrier((total_grad, gated_window))
    adjoint = jnp.einsum("gau,sugc->sagc", bwd_band, gated_window, preferred_element_type=jnp.float32)
    dmixed = adjoint.reshape(rows, channels).astype(jnp.bfloat16)
    squares = radix_round(jnp.sum(total_grad * total_grad), "chan", 1, 2)
    squares, late_query, late_key, late_value, late_grad = lax.optimization_barrier(
        (squares, query_rows, key_rows, value_rows, grad_rows)
    )
    squares = radix_round(squares, "chan", 0)
    limit = math.sqrt(groups * lax.axis_size("chan") * taps)
    factor = jnp.minimum(1.0, limit / jnp.sqrt(squares + 1e-06))
    filter_grad = factor * total_grad

    gated_out = times_rounded(late_query, convolved)
    grad_query = times_rounded(late_grad, convolved)
    grad_key = times_rounded(dmixed, late_value)
    grad_value = times_rounded(dmixed, late_key)
    return (gated_out, grad_query, grad_key, grad_value, filter_grad)


def _bwd_select(taps, out_rows, window):
    j = lax.broadcasted_iota(jnp.int32, (taps, out_rows, window), 0)
    a = lax.broadcasted_iota(jnp.int32, (taps, out_rows, window), 1)
    u = lax.broadcasted_iota(jnp.int32, (taps, out_rows, window), 2)
    return (u == a + j).astype(jnp.bfloat16)


def solution(mesh):
    return jax.shard_map(
        shards,
        mesh=mesh,
        in_specs=(
            P("seq", "chan"),
            P("seq", "chan"),
            P("seq", "chan"),
            P("seq", "chan"),
            P("chan", None),
            P(),
        ),
        out_specs=(
            P("seq", "chan"),
            P("seq", "chan"),
            P("seq", "chan"),
            P("seq", "chan"),
            P("chan", None),
        ),
        check_vma=False,
    )
```

```python
import math

import jax
import jax.numpy as jnp
from jax import lax
from jax.experimental import pallas as pl
from jax.experimental.pallas import tpu as pltpu
from jax.sharding import PartitionSpec as P


def times_rounded(left, right):
    return (left.astype(jnp.float32) * right.astype(jnp.float32)).astype(jnp.bfloat16)


def swap(value, axis, mask):
    size = lax.axis_size(axis)
    return lax.ppermute(value, axis, [(i, i ^ mask) for i in range(size)])


def radix_round(value, axis, low, high=None):
    if high is None:
        return value + swap(value, axis, 1 << low)
    one, two = 1 << low, 1 << high
    return (value + swap(value, axis, one)) + (swap(value, axis, two) + swap(value, axis, one | two))


def butterfly_sum(value, axis, rounds):
    for bits in rounds:
        value = radix_round(value, axis, *bits)
    return value


def _take_kernel(slots_ref, blocks_ref, out_ref, sems):
    count = out_ref.shape[0]
    copies = [
        pltpu.make_async_copy(blocks_ref.at[slots_ref[n]], out_ref.at[n], sems.at[n]) for n in range(count)
    ]
    for copy in copies:
        copy.start()
    for copy in copies:
        copy.wait()


def take_blocks(blocks, slots):
    count = slots.shape[0]
    block_bytes = blocks.shape[1] * blocks.shape[2] * blocks.dtype.itemsize
    return pl.pallas_call(
        _take_kernel,
        out_shape=jax.ShapeDtypeStruct((count,) + blocks.shape[1:], blocks.dtype),
        in_specs=[pl.BlockSpec(memory_space=pltpu.SMEM), pl.BlockSpec(memory_space=pl.ANY)],
        out_specs=pl.BlockSpec(memory_space=pltpu.VMEM),
        scratch_shapes=[pltpu.SemaphoreType.DMA((count,))],
        cost_estimate=pl.CostEstimate(flops=0, bytes_accessed=2 * count * block_bytes, transcendentals=0),
    )(slots, blocks)


def band_select(taps, out_rows, window, lead):
    j = lax.broadcasted_iota(jnp.int32, (taps, out_rows, window), 0)
    a = lax.broadcasted_iota(jnp.int32, (taps, out_rows, window), 1)
    w = lax.broadcasted_iota(jnp.int32, (taps, out_rows, window), 2)
    return (w == lead + a - j).astype(jnp.bfloat16)


def shards(query_rows, key_rows, value_rows, grad_rows, filters, span_order):
    device = lax.axis_index("seq")
    devices = lax.axis_size("seq")
    rows, channels = query_rows.shape
    spans = span_order.shape[0]
    span_rows = rows * devices // spans
    per_device = rows // span_rows
    taps = filters.shape[1]
    groups = filters.shape[0]
    group_size = channels // groups
    halo = -(-(taps - 1) // span_rows)
    lead = halo * span_rows
    window = lead + span_rows

    mixed = times_rounded(key_rows, value_rows)
    gated = times_rounded(grad_rows, query_rows)
    gathered = lax.all_gather(jnp.stack([mixed, gated]), "seq", axis=0, tiled=False)
    blocks = gathered.reshape(devices * 2 * per_device, span_rows, channels)

    slot_of = jnp.zeros((spans,), jnp.int32).at[span_order].set(jnp.arange(spans, dtype=jnp.int32))
    mine = lax.dynamic_slice_in_dim(span_order, device * per_device, per_device)
    step = jnp.arange(halo, dtype=jnp.int32)
    before = mine[:, None] - halo + step[None, :]
    after = mine[:, None] + 1 + step[None, :]

    def pick(blocks, which, wanted):
        valid = (wanted >= 0) & (wanted < spans)
        slots = slot_of[jnp.clip(wanted, 0, spans - 1)].reshape(-1)
        slots = ((slots // per_device) * 2 + which) * per_device + slots % per_device
        taken = take_blocks(blocks, slots).reshape(per_device, halo, span_rows, channels)
        return jnp.where(valid[:, :, None, None], taken, jnp.zeros_like(taken))

    own_mixed = mixed.reshape(per_device, span_rows, channels)
    own_gated = gated.reshape(per_device, span_rows, channels)
    mixed_window = jnp.concatenate(
        [pick(blocks, 0, before).reshape(per_device, lead, channels), own_mixed], axis=1
    )
    mixed_window = mixed_window.reshape(per_device, window, groups, group_size)

    select_fwd = band_select(taps, span_rows, window, lead)
    fwd_band = jnp.einsum(
        "gj,jaw->gaw", filters, select_fwd, preferred_element_type=jnp.float32
    ).astype(jnp.bfloat16)
    bwd_band = jnp.einsum(
        "gj,jau->gau", filters, _bwd_select(taps, span_rows, window),
        preferred_element_type=jnp.float32,
    ).astype(jnp.bfloat16)

    conv = jnp.einsum("gaw,swgc->sagc", fwd_band, mixed_window, preferred_element_type=jnp.float32)
    convolved = conv.reshape(rows, channels).astype(jnp.bfloat16)
    own_gated_g = own_gated.reshape(per_device, span_rows, groups, group_size)
    corr = jnp.einsum(
        "sagc,swgc->gaw", own_gated_g, mixed_window, preferred_element_type=jnp.float32
    )
    partial_grad = jnp.einsum(
        "gaw,jaw->gj", corr, select_fwd.astype(jnp.float32), precision=lax.Precision.HIGH
    )
    seq_rounds = ((0, 3), (1, 2))
    total_grad = radix_round(partial_grad, "seq", *seq_rounds[0])
    total_grad, late_blocks = lax.optimization_barrier((total_grad, blocks))
    gated_window = jnp.concatenate(
        [own_gated, pick(late_blocks, 1, after).reshape(per_device, lead, channels)], axis=1
    ).reshape(per_device, window, groups, group_size)
    total_grad = butterfly_sum(total_grad, "seq", seq_rounds[1:])
    total_grad, gated_window = lax.optimization_barrier((total_grad, gated_window))
    adjoint = jnp.einsum("gau,sugc->sagc", bwd_band, gated_window, preferred_element_type=jnp.float32)
    dmixed = adjoint.reshape(rows, channels).astype(jnp.bfloat16)
    squares = radix_round(jnp.sum(total_grad * total_grad), "chan", 1, 2)
    squares, late_query, late_key, late_value, late_grad = lax.optimization_barrier(
        (squares, query_rows, key_rows, value_rows, grad_rows)
    )
    squares = radix_round(squares, "chan", 0)
    limit = math.sqrt(groups * lax.axis_size("chan") * taps)
    factor = jnp.minimum(1.0, limit / jnp.sqrt(squares + 1e-06))
    filter_grad = factor * total_grad

    gated_out = times_rounded(late_query, convolved)
    grad_query = times_rounded(late_grad, convolved)
    grad_key = times_rounded(dmixed, late_value)
    grad_value = times_rounded(dmixed, late_key)
    return (gated_out, grad_query, grad_key, grad_value, filter_grad)


def _bwd_select(taps, out_rows, window):
    j = lax.broadcasted_iota(jnp.int32, (taps, out_rows, window), 0)
    a = lax.broadcasted_iota(jnp.int32, (taps, out_rows, window), 1)
    u = lax.broadcasted_iota(jnp.int32, (taps, out_rows, window), 2)
    return (u == a + j).astype(jnp.bfloat16)


def solution(mesh):
    return jax.shard_map(
        shards,
        mesh=mesh,
        in_specs=(
            P("seq", "chan"),
            P("seq", "chan"),
            P("seq", "chan"),
            P("seq", "chan"),
            P("chan", None),
            P(),
        ),
        out_specs=(
            P("seq", "chan"),
            P("seq", "chan"),
            P("seq", "chan"),
            P("seq", "chan"),
            P("chan", None),
        ),
        check_vma=False,
    )
```

```python
import functools
import math

import jax
import jax.numpy as jnp
from jax import lax
from jax.experimental import pallas as pl
from jax.experimental.pallas import tpu as pltpu
from jax.sharding import PartitionSpec as P


def times_rounded(left, right):
    return (left.astype(jnp.float32) * right.astype(jnp.float32)).astype(jnp.bfloat16)


def swap(value, axis, mask):
    size = lax.axis_size(axis)
    return lax.ppermute(value, axis, [(i, i ^ mask) for i in range(size)])


def radix_round(value, axis, low, high=None):
    if high is None:
        return value + swap(value, axis, 1 << low)
    one, two = 1 << low, 1 << high
    return (value + swap(value, axis, one)) + (swap(value, axis, two) + swap(value, axis, one | two))


def butterfly_sum(value, axis, rounds):
    for bits in rounds:
        value = radix_round(value, axis, *bits)
    return value


def _window_kernel(own_first, slots_ref, blocks_ref, own_ref, out_ref, sems):
    spans, rows = own_ref.shape[0], own_ref.shape[1]
    halo = slots_ref.shape[0] // spans
    copies = []
    for s in range(spans):
        own_at = 0 if own_first else halo * rows
        first = rows if own_first else 0
        copies.append(pltpu.make_async_copy(
            own_ref.at[s], out_ref.at[s, pl.ds(own_at, rows)], sems.at[s * (halo + 1)]))
        for h in range(halo):
            copies.append(pltpu.make_async_copy(
                blocks_ref.at[slots_ref[s * halo + h]],
                out_ref.at[s, pl.ds(first + h * rows, rows)],
                sems.at[s * (halo + 1) + 1 + h],
            ))
    for copy in copies:
        copy.start()
    for copy in copies:
        copy.wait()


def build_window(blocks, own, slots, own_first):
    spans, rows, channels = own.shape
    halo = slots.shape[0] // spans
    window_bytes = spans * (halo + 1) * rows * channels * own.dtype.itemsize
    return pl.pallas_call(
        functools.partial(_window_kernel, own_first),
        out_shape=jax.ShapeDtypeStruct((spans, (halo + 1) * rows, channels), own.dtype),
        in_specs=[
            pl.BlockSpec(memory_space=pltpu.SMEM),
            pl.BlockSpec(memory_space=pl.ANY),
            pl.BlockSpec(memory_space=pl.ANY),
        ],
        out_specs=pl.BlockSpec(memory_space=pltpu.VMEM),
        scratch_shapes=[pltpu.SemaphoreType.DMA((spans * (halo + 1),))],
        cost_estimate=pl.CostEstimate(flops=0, bytes_accessed=2 * window_bytes, transcendentals=0),
    )(slots, blocks, own)


def band_select(taps, out_rows, window, lead):
    j = lax.broadcasted_iota(jnp.int32, (taps, out_rows, window), 0)
    a = lax.broadcasted_iota(jnp.int32, (taps, out_rows, window), 1)
    w = lax.broadcasted_iota(jnp.int32, (taps, out_rows, window), 2)
    return (w == lead + a - j).astype(jnp.bfloat16)


def shards(query_rows, key_rows, value_rows, grad_rows, filters, span_order):
    device = lax.axis_index("seq")
    devices = lax.axis_size("seq")
    rows, channels = query_rows.shape
    spans = span_order.shape[0]
    span_rows = rows * devices // spans
    per_device = rows // span_rows
    taps = filters.shape[1]
    groups = filters.shape[0]
    group_size = channels // groups
    halo = -(-(taps - 1) // span_rows)
    lead = halo * span_rows
    window = lead + span_rows

    mixed = times_rounded(key_rows, value_rows)
    gated = times_rounded(grad_rows, query_rows)
    gathered = lax.all_gather(jnp.stack([mixed, gated]), "seq", axis=0, tiled=False)
    blocks = gathered.reshape(devices * 2 * per_device, span_rows, channels)

    slot_of = jnp.zeros((spans,), jnp.int32).at[span_order].set(jnp.arange(spans, dtype=jnp.int32))
    mine = lax.dynamic_slice_in_dim(span_order, device * per_device, per_device)
    step = jnp.arange(halo, dtype=jnp.int32)
    before = mine[:, None] - halo + step[None, :]
    after = mine[:, None] + 1 + step[None, :]

    def pick(blocks, which, wanted, own, own_first):
        valid = (wanted >= 0) & (wanted < spans)
        slots = slot_of[jnp.clip(wanted, 0, spans - 1)].reshape(-1)
        slots = ((slots // per_device) * 2 + which) * per_device + slots % per_device
        window_rows = build_window(blocks, own, slots, own_first)
        keep = jnp.concatenate([jnp.ones((per_device, 1), bool), valid], axis=1) if own_first else (
            jnp.concatenate([valid, jnp.ones((per_device, 1), bool)], axis=1))
        keep = jnp.repeat(keep, span_rows, axis=1)
        return jnp.where(keep[:, :, None], window_rows, jnp.zeros_like(window_rows)).reshape(
            per_device, window, groups, group_size
        )

    own_mixed = mixed.reshape(per_device, span_rows, channels)
    own_gated = gated.reshape(per_device, span_rows, channels)
    mixed_window = pick(blocks, 0, before, own_mixed, False)

    select_fwd = band_select(taps, span_rows, window, lead)
    fwd_band = jnp.einsum(
        "gj,jaw->gaw", filters, select_fwd, preferred_element_type=jnp.float32
    ).astype(jnp.bfloat16)
    bwd_band = jnp.einsum(
        "gj,jau->gau", filters, _bwd_select(taps, span_rows, window),
        preferred_element_type=jnp.float32,
    ).astype(jnp.bfloat16)

    conv = jnp.einsum("gaw,swgc->sagc", fwd_band, mixed_window, preferred_element_type=jnp.float32)
    convolved = conv.reshape(rows, channels).astype(jnp.bfloat16)
    own_gated_g = own_gated.reshape(per_device, span_rows, groups, group_size)
    corr = jnp.einsum(
        "sagc,swgc->gaw", own_gated_g, mixed_window, preferred_element_type=jnp.float32
    )
    partial_grad = jnp.einsum(
        "gaw,jaw->gj", corr, select_fwd.astype(jnp.float32), precision=lax.Precision.HIGH
    )
    seq_rounds = ((0, 3), (1, 2))
    total_grad = radix_round(partial_grad, "seq", *seq_rounds[0])
    total_grad, late_blocks = lax.optimization_barrier((total_grad, blocks))
    gated_window = pick(late_blocks, 1, after, own_gated, True)
    total_grad = butterfly_sum(total_grad, "seq", seq_rounds[1:])
    total_grad, gated_window = lax.optimization_barrier((total_grad, gated_window))
    adjoint = jnp.einsum("gau,sugc->sagc", bwd_band, gated_window, preferred_element_type=jnp.float32)
    dmixed = adjoint.reshape(rows, channels).astype(jnp.bfloat16)
    squares = radix_round(jnp.sum(total_grad * total_grad), "chan", 1, 2)
    squares, late_query, late_key, late_value, late_grad = lax.optimization_barrier(
        (squares, query_rows, key_rows, value_rows, grad_rows)
    )
    squares = radix_round(squares, "chan", 0)
    limit = math.sqrt(groups * lax.axis_size("chan") * taps)
    factor = jnp.minimum(1.0, limit / jnp.sqrt(squares + 1e-06))
    filter_grad = factor * total_grad

    gated_out = times_rounded(late_query, convolved)
    grad_query = times_rounded(late_grad, convolved)
    grad_key = times_rounded(dmixed, late_value)
    grad_value = times_rounded(dmixed, late_key)
    return (gated_out, grad_query, grad_key, grad_value, filter_grad)


def _bwd_select(taps, out_rows, window):
    j = lax.broadcasted_iota(jnp.int32, (taps, out_rows, window), 0)
    a = lax.broadcasted_iota(jnp.int32, (taps, out_rows, window), 1)
    u = lax.broadcasted_iota(jnp.int32, (taps, out_rows, window), 2)
    return (u == a + j).astype(jnp.bfloat16)


def solution(mesh):
    return jax.shard_map(
        shards,
        mesh=mesh,
        in_specs=(
            P("seq", "chan"),
            P("seq", "chan"),
            P("seq", "chan"),
            P("seq", "chan"),
            P("chan", None),
            P(),
        ),
        out_specs=(
            P("seq", "chan"),
            P("seq", "chan"),
            P("seq", "chan"),
            P("seq", "chan"),
            P("chan", None),
        ),
        check_vma=False,
    )
```

```python
import math

import jax
import jax.numpy as jnp
from jax import lax
from jax.experimental import pallas as pl
from jax.experimental.pallas import tpu as pltpu
from jax.sharding import PartitionSpec as P


def times_rounded(left, right):
    return (left.astype(jnp.float32) * right.astype(jnp.float32)).astype(jnp.bfloat16)


def swap(value, axis, mask):
    size = lax.axis_size(axis)
    return lax.ppermute(value, axis, [(i, i ^ mask) for i in range(size)])


def radix_round(value, axis, low, high=None):
    if high is None:
        return value + swap(value, axis, 1 << low)
    one, two = 1 << low, 1 << high
    return (value + swap(value, axis, one)) + (swap(value, axis, two) + swap(value, axis, one | two))


def butterfly_sum(value, axis, rounds):
    for bits in rounds:
        value = radix_round(value, axis, *bits)
    return value


def _take_kernel(slots_ref, blocks_ref, out_ref, sems):
    count = out_ref.shape[0]
    copies = [
        pltpu.make_async_copy(blocks_ref.at[slots_ref[n]], out_ref.at[n], sems.at[n]) for n in range(count)
    ]
    for copy in copies:
        copy.start()
    for copy in copies:
        copy.wait()


def take_blocks(blocks, slots):
    count = slots.shape[0]
    block_bytes = blocks.shape[1] * blocks.shape[2] * blocks.dtype.itemsize
    return pl.pallas_call(
        _take_kernel,
        out_shape=jax.ShapeDtypeStruct((count,) + blocks.shape[1:], blocks.dtype),
        in_specs=[pl.BlockSpec(memory_space=pltpu.SMEM), pl.BlockSpec(memory_space=pl.ANY)],
        out_specs=pl.BlockSpec(memory_space=pltpu.VMEM),
        scratch_shapes=[pltpu.SemaphoreType.DMA((count,))],
        cost_estimate=pl.CostEstimate(flops=0, bytes_accessed=2 * count * block_bytes, transcendentals=0),
    )(slots, blocks)


def band_select(taps, out_rows, window, lead):
    j = lax.broadcasted_iota(jnp.int32, (taps, out_rows, window), 0)
    a = lax.broadcasted_iota(jnp.int32, (taps, out_rows, window), 1)
    w = lax.broadcasted_iota(jnp.int32, (taps, out_rows, window), 2)
    return (w == lead + a - j).astype(jnp.bfloat16)


def shards(query_rows, key_rows, value_rows, grad_rows, filters, span_order):
    device = lax.axis_index("seq")
    devices = lax.axis_size("seq")
    rows, channels = query_rows.shape
    spans = span_order.shape[0]
    span_rows = rows * devices // spans
    per_device = rows // span_rows
    taps = filters.shape[1]
    groups = filters.shape[0]
    group_size = channels // groups
    halo = -(-(taps - 1) // span_rows)
    lead = halo * span_rows
    window = lead + span_rows

    mixed = times_rounded(key_rows, value_rows)
    gated = times_rounded(grad_rows, query_rows)
    gathered = lax.all_gather(jnp.stack([mixed, gated]), "seq", axis=0, tiled=False)
    blocks = gathered.reshape(devices * 2 * per_device, span_rows, channels)

    slot_of = jnp.zeros((spans,), jnp.int32).at[span_order].set(jnp.arange(spans, dtype=jnp.int32))
    mine = lax.dynamic_slice_in_dim(span_order, device * per_device, per_device)
    step = jnp.arange(halo, dtype=jnp.int32)
    before = mine[:, None] - halo + step[None, :]
    after = mine[:, None] + 1 + step[None, :]

    def pick(blocks, which, wanted):
        valid = (wanted >= 0) & (wanted < spans)
        slots = slot_of[jnp.clip(wanted, 0, spans - 1)].reshape(-1)
        slots = ((slots // per_device) * 2 + which) * per_device + slots % per_device
        taken = take_blocks(blocks, slots).reshape(per_device, halo, span_rows, channels)
        return jnp.where(valid[:, :, None, None], taken, jnp.zeros_like(taken))

    own_mixed = mixed.reshape(per_device, span_rows, channels)
    own_gated = gated.reshape(per_device, span_rows, channels)
    mixed_window = jnp.concatenate(
        [pick(blocks, 0, before).reshape(per_device, lead, channels), own_mixed], axis=1
    )
    mixed_window = mixed_window.reshape(per_device, window, groups, group_size)

    select_fwd = band_select(taps, span_rows, window, lead)
    fwd_band = jnp.einsum(
        "gj,jaw->gaw", filters, select_fwd, preferred_element_type=jnp.float32
    ).astype(jnp.bfloat16)
    bwd_band = jnp.einsum(
        "gj,jau->gau", filters, _bwd_select(taps, span_rows, window),
        preferred_element_type=jnp.float32,
    ).astype(jnp.bfloat16)

    conv = jnp.einsum("gaw,swgc->sagc", fwd_band, mixed_window, preferred_element_type=jnp.float32)
    convolved = conv.reshape(rows, channels).astype(jnp.bfloat16)
    own_gated_g = own_gated.reshape(per_device, span_rows, groups, group_size)
    def lag_sums(source, select):
        corr = jnp.einsum("sagc,swgc->gaw", own_gated_g, source, preferred_element_type=jnp.float32)
        return jnp.einsum("gaw,jaw->gj", corr, select.astype(jnp.float32), precision=lax.Precision.HIGH)

    own_lags = lag_sums(own_mixed.reshape(per_device, span_rows, groups, group_size), select_fwd[:, :, lead:])
    partial_grad = lag_sums(mixed_window[:, :lead], select_fwd[:, :, :lead]) + own_lags
    seq_rounds = ((0, 3), (1, 2))
    total_grad = radix_round(partial_grad, "seq", *seq_rounds[0])
    total_grad, late_blocks = lax.optimization_barrier((total_grad, blocks))
    gated_window = jnp.concatenate(
        [own_gated, pick(late_blocks, 1, after).reshape(per_device, lead, channels)], axis=1
    ).reshape(per_device, window, groups, group_size)
    total_grad = butterfly_sum(total_grad, "seq", seq_rounds[1:])
    total_grad, gated_window = lax.optimization_barrier((total_grad, gated_window))
    adjoint = jnp.einsum("gau,sugc->sagc", bwd_band, gated_window, preferred_element_type=jnp.float32)
    dmixed = adjoint.reshape(rows, channels).astype(jnp.bfloat16)
    squares = radix_round(jnp.sum(total_grad * total_grad), "chan", 1, 2)
    squares, late_query, late_key, late_value, late_grad = lax.optimization_barrier(
        (squares, query_rows, key_rows, value_rows, grad_rows)
    )
    squares = radix_round(squares, "chan", 0)
    limit = math.sqrt(groups * lax.axis_size("chan") * taps)
    factor = jnp.minimum(1.0, limit / jnp.sqrt(squares + 1e-06))
    filter_grad = factor * total_grad

    gated_out = times_rounded(late_query, convolved)
    grad_query = times_rounded(late_grad, convolved)
    grad_key = times_rounded(dmixed, late_value)
    grad_value = times_rounded(dmixed, late_key)
    return (gated_out, grad_query, grad_key, grad_value, filter_grad)


def _bwd_select(taps, out_rows, window):
    j = lax.broadcasted_iota(jnp.int32, (taps, out_rows, window), 0)
    a = lax.broadcasted_iota(jnp.int32, (taps, out_rows, window), 1)
    u = lax.broadcasted_iota(jnp.int32, (taps, out_rows, window), 2)
    return (u == a + j).astype(jnp.bfloat16)


def solution(mesh):
    return jax.shard_map(
        shards,
        mesh=mesh,
        in_specs=(
            P("seq", "chan"),
            P("seq", "chan"),
            P("seq", "chan"),
            P("seq", "chan"),
            P("chan", None),
            P(),
        ),
        out_specs=(
            P("seq", "chan"),
            P("seq", "chan"),
            P("seq", "chan"),
            P("seq", "chan"),
            P("chan", None),
        ),
        check_vma=False,
    )
```

```python
import math

import jax
import jax.numpy as jnp
from jax import lax
from jax.experimental import pallas as pl
from jax.experimental.pallas import tpu as pltpu
from jax.sharding import PartitionSpec as P


def times_rounded(left, right):
    return (left.astype(jnp.float32) * right.astype(jnp.float32)).astype(jnp.bfloat16)


def swap(value, axis, mask):
    size = lax.axis_size(axis)
    return lax.ppermute(value, axis, [(i, i ^ mask) for i in range(size)])


def radix_round(value, axis, low, high=None):
    if high is None:
        return value + swap(value, axis, 1 << low)
    one, two = 1 << low, 1 << high
    return (value + swap(value, axis, one)) + (swap(value, axis, two) + swap(value, axis, one | two))


def butterfly_sum(value, axis, rounds):
    for bits in rounds:
        value = radix_round(value, axis, *bits)
    return value


def _take_kernel(slots_ref, blocks_ref, out_ref, sems):
    count = out_ref.shape[0]
    copies = [
        pltpu.make_async_copy(blocks_ref.at[slots_ref[n]], out_ref.at[n], sems.at[n]) for n in range(count)
    ]
    for copy in copies:
        copy.start()
    for copy in copies:
        copy.wait()


def take_blocks(blocks, slots):
    count = slots.shape[0]
    block_bytes = blocks.shape[1] * blocks.shape[2] * blocks.dtype.itemsize
    return pl.pallas_call(
        _take_kernel,
        out_shape=jax.ShapeDtypeStruct((count,) + blocks.shape[1:], blocks.dtype),
        in_specs=[pl.BlockSpec(memory_space=pltpu.SMEM), pl.BlockSpec(memory_space=pl.ANY)],
        out_specs=pl.BlockSpec(memory_space=pltpu.VMEM),
        scratch_shapes=[pltpu.SemaphoreType.DMA((count,))],
        cost_estimate=pl.CostEstimate(flops=0, bytes_accessed=2 * count * block_bytes, transcendentals=0),
    )(slots, blocks)


def band_select(taps, out_rows, window, lead):
    j = lax.broadcasted_iota(jnp.int32, (taps, out_rows, window), 0)
    a = lax.broadcasted_iota(jnp.int32, (taps, out_rows, window), 1)
    w = lax.broadcasted_iota(jnp.int32, (taps, out_rows, window), 2)
    return (w == lead + a - j).astype(jnp.bfloat16)


def shards(query_rows, key_rows, value_rows, grad_rows, filters, span_order):
    device = lax.axis_index("seq")
    devices = lax.axis_size("seq")
    rows, channels = query_rows.shape
    spans = span_order.shape[0]
    span_rows = rows * devices // spans
    per_device = rows // span_rows
    taps = filters.shape[1]
    groups = filters.shape[0]
    group_size = channels // groups
    halo = -(-(taps - 1) // span_rows)
    lead = halo * span_rows
    window = lead + span_rows

    mixed = times_rounded(key_rows, value_rows)
    gated = times_rounded(grad_rows, query_rows)
    gathered = lax.all_gather(jnp.stack([mixed, gated]), "seq", axis=0, tiled=False)
    blocks = gathered.reshape(devices * 2 * per_device, span_rows, channels)

    slot_of = jnp.zeros((spans,), jnp.int32).at[span_order].set(jnp.arange(spans, dtype=jnp.int32))
    mine = lax.dynamic_slice_in_dim(span_order, device * per_device, per_device)
    step = jnp.arange(halo, dtype=jnp.int32)
    before = mine[:, None] - halo + step[None, :]
    after = mine[:, None] + 1 + step[None, :]

    def pick(blocks, which, wanted):
        valid = (wanted >= 0) & (wanted < spans)
        slots = slot_of[jnp.clip(wanted, 0, spans - 1)].reshape(-1)
        slots = ((slots // per_device) * 2 + which) * per_device + slots % per_device
        taken = take_blocks(blocks, slots).reshape(per_device, halo, span_rows, channels)
        return jnp.where(valid[:, :, None, None], taken, jnp.zeros_like(taken))

    own_mixed = mixed.reshape(per_device, span_rows, channels)
    own_gated = gated.reshape(per_device, span_rows, channels)
    mixed_window = jnp.concatenate(
        [pick(blocks, 0, before).reshape(per_device, lead, channels), own_mixed], axis=1
    )
    mixed_window = mixed_window.reshape(per_device, window, groups, group_size)

    select_fwd = band_select(taps, span_rows, window, lead)
    fwd_band = jnp.einsum(
        "gj,jaw->gaw", filters, select_fwd, preferred_element_type=jnp.float32
    ).astype(jnp.bfloat16)
    bwd_band = jnp.einsum(
        "gj,jau->gau", filters, _bwd_select(taps, span_rows, window),
        preferred_element_type=jnp.float32,
    ).astype(jnp.bfloat16)

    conv = jnp.einsum("gaw,swgc->sagc", fwd_band, mixed_window, preferred_element_type=jnp.float32)
    convolved = conv.reshape(rows, channels).astype(jnp.bfloat16)
    own_gated_g = own_gated.reshape(per_device, span_rows, groups, group_size)
    corr = jnp.einsum(
        "sagc,swgc->gaw", own_gated_g, mixed_window, preferred_element_type=jnp.float32
    )
    partial_grad = jnp.einsum(
        "gaw,jaw->gj", corr, select_fwd.astype(jnp.float32), precision=lax.Precision.HIGH
    )
    seq_rounds = ((0, 3), (1, 2))
    total_grad = radix_round(partial_grad, "seq", *seq_rounds[0])
    total_grad, late_blocks = lax.optimization_barrier((total_grad, blocks))
    gated_window = jnp.concatenate(
        [own_gated, pick(late_blocks, 1, after).reshape(per_device, lead, channels)], axis=1
    ).reshape(per_device, window, groups, group_size)
    total_grad = butterfly_sum(total_grad, "seq", seq_rounds[1:])
    total_grad, gated_window = lax.optimization_barrier((total_grad, gated_window))
    adjoint = jnp.einsum("gau,sugc->sagc", bwd_band, gated_window, preferred_element_type=jnp.float32)
    dmixed = adjoint.reshape(rows, channels).astype(jnp.bfloat16)
    squares = butterfly_sum(jnp.sum(total_grad * total_grad), "chan", ((1,), (2,)))
    squares, late_query, late_key, late_value, late_grad = lax.optimization_barrier(
        (squares, query_rows, key_rows, value_rows, grad_rows)
    )
    squares = radix_round(squares, "chan", 0)
    limit = math.sqrt(groups * lax.axis_size("chan") * taps)
    factor = jnp.minimum(1.0, limit / jnp.sqrt(squares + 1e-06))
    filter_grad = factor * total_grad

    gated_out = times_rounded(late_query, convolved)
    grad_query = times_rounded(late_grad, convolved)
    grad_key = times_rounded(dmixed, late_value)
    grad_value = times_rounded(dmixed, late_key)
    return (gated_out, grad_query, grad_key, grad_value, filter_grad)


def _bwd_select(taps, out_rows, window):
    j = lax.broadcasted_iota(jnp.int32, (taps, out_rows, window), 0)
    a = lax.broadcasted_iota(jnp.int32, (taps, out_rows, window), 1)
    u = lax.broadcasted_iota(jnp.int32, (taps, out_rows, window), 2)
    return (u == a + j).astype(jnp.bfloat16)


def solution(mesh):
    return jax.shard_map(
        shards,
        mesh=mesh,
        in_specs=(
            P("seq", "chan"),
            P("seq", "chan"),
            P("seq", "chan"),
            P("seq", "chan"),
            P("chan", None),
            P(),
        ),
        out_specs=(
            P("seq", "chan"),
            P("seq", "chan"),
            P("seq", "chan"),
            P("seq", "chan"),
            P("chan", None),
        ),
        check_vma=False,
    )
```
